32 devices in a mesh: cp: 2 (over y), tp: 4 (over x, core), ep: 4 (over z).
Axes of the slice: x: 2, y: 2, z: 4, core: 2. Of those that a mesh axis runs over, the one named last changes fastest.
Arguments:
- query: bfloat16 [8, 512, 4096], P('ep', 'cp', 'tp'), may hold values from -6 to 6
- keys: bfloat16 [8, 512, 512], P('ep', 'cp', 'tp'), may hold values from -6 to 6
- values: bfloat16 [8, 512, 512], P('ep', 'cp', 'tp'), may hold values from -24 to 24
- segment_ids: int32 [8, 512], P('ep', 'cp'), may hold values from 0 to 3, never falling along the last dimension, each value on 1 to 256 neighbouring positions
- query_norm_gain: float32 [128], replicated, may hold values from 0.25 to 1.75
- key_norm_gain: float32 [128], replicated, may hold values from 0.25 to 1.75
- out_weight: bfloat16 [4096, 2048], P('tp', 'cp'), may hold values from -0.09375 to 0.09375
- residual: bfloat16 [8, 512, 2048], P('ep', 'cp'), may hold values from -3 to 3
- norm_gain: float32 [2048], replicated, may hold values from 0.25 to 1.75
- router_weight: bfloat16 [2048, 16], replicated, may hold values from -0.125 to 0.125
- expert_ids: int32 [8, 512, 8], P('ep', 'cp'), may hold values from 0 to 15, all different within a row; in each aligned block of 64 rows (0 to 63, 64 to 127, ..., all dimensions but the last counted through in order) at most 36 rows name the same one
- expert_gate: bfloat16 [16, 2048, 768], P(('tp', 'ep'), None, 'cp'), may hold values from -0.125 to 0.125
- expert_up: bfloat16 [16, 2048, 768], P(('tp', 'ep'), None, 'cp'), may hold values from -0.125 to 0.125
- expert_down: bfloat16 [16, 2048, 768], P(('tp', 'ep'), None, 'cp'), may hold values from -0.21875 to 0.21875
Outputs:
- layer_out: bfloat16 [8, 512, 2048], P('ep', ('cp', 'tp'))
The draws below stay inside these ranges and needn't reach their ends.
Inputs may be any that keep to these rules, and one draw needn't show every extreme that they name: `segment_ids`: document numbers never fall along a sequence. `expert_ids`: each token names 8 different experts; in every aligned block of 64 positions of a sequence no expert is named by more than 36 tokens, a bound that some block reaches.
All inputs are finite; a program needn't handle non-finite values.
Results may differ from the reference program's by a relative error of at most 0.007.
Values may be sent and summed in bfloat16 or wider, within the bound.
No kernel may reach another device: no remote copies, remote signals or barrier semaphores. Data moves between devices by JAX's collectives and lax.ppermute only.
A program may use at most 128 MiB of HBM per device.

```python
import math
import jax
import jax.numpy as jnp
import numpy as np
from jax import lax

D = 2048
FF = 768
QUERY_HEADS = 32
KEY_VALUE_HEADS = 4
HEAD_WIDTH = 128
TOP = 8
PACKED_LENGTH = 512
PACKED_SEQUENCES = 8
EXPERTS = 16
MOE_DEV = 64
CAP = 36


def steps_of(rng, shape, pieces, smallest, high):
    level = 1.0
    for dim, parts in pieces:
        draws = jax.random.uniform(jax.random.fold_in(jax.random.fold_in(rng, 6), dim), (parts,), jnp.float32, smallest / len(pieces), high / len(pieces))
        level = level * jnp.repeat(jnp.exp(draws), shape[dim] // parts).reshape((-1,) + (1,) * (len(shape) - 1 - dim))
    return level


def profile(number_of, total, most, slope):
    portions = [(1 << 20) // math.isqrt(standing ** slope) + 1 for standing in range(2, number_of + 1)]
    rest, given = total - most - (number_of - 1), [1] * (number_of - 1)
    while rest > 0:
        candidates = [i for i in range(number_of - 1) if given[i] < most]
        pool, left = sum([portions[i] for i in candidates]), rest
        for i in candidates:
            addition = min(most - given[i], max(1, left * portions[i] // pool), rest)
            given[i] = given[i] + addition
            rest = rest - addition
    return np.array([most] + given)


def uneven(own_key, count, total, reach, lean):
    if count == 2:
        one = jax.random.randint(own_key, (), max(1, total - reach), min(reach, total - 1) + 1)
        return jnp.stack([one, total - one])
    lengths = jnp.asarray(profile(count, total, reach, lean), jnp.int32)
    pairs = (count - 1) // 2
    donor, sink = lengths[1:1 + 2 * pairs:2], lengths[2:2 + 2 * pairs:2]
    slack = jnp.minimum(donor - 1, reach - sink)
    passed = jax.random.randint(jax.random.fold_in(own_key, 1), (pairs,), 0, 1 << 20) % (slack + 1)
    lengths = lengths.at[1:1 + 2 * pairs:2].set(donor - passed).at[2:2 + 2 * pairs:2].set(sink + passed)
    return lengths[jax.random.permutation(jax.random.fold_in(own_key, 2), count)]


def shared_out(rng, own, number, rows, count, top, reach, slope):
    sequence = jax.random.permutation(rng, count)
    crowded, ordinary = load_shares(count, rows * top, reach, slope, True), load_shares(count, rows * top, reach, slope, False)
    places = jnp.arange(count)

    def named(lengths, turn):
        used = int((lengths > 0).sum())
        fixed = max(1, used // 4)
        passed = fixed + (places - fixed + turn * (used - fixed)) % max(1, count - fixed)
        return jnp.zeros((count,), jnp.int32).at[sequence[jnp.where(places < fixed, places, passed)]].set(jnp.asarray(lengths, jnp.int32))

    lengths = jnp.where(number % 4 == 0, named(crowded, number // 4), named(ordinary, number - number // 4 - 1))
    mixed = jax.random.permutation(jax.random.fold_in(own, 3), count)
    giver, sink = mixed[0:count // 2 * 2:2], mixed[1:count // 2 * 2:2]
    slack = jnp.minimum(lengths[giver] - 1, reach - lengths[sink]) // 2
    slack = jnp.where((giver == sequence[0]) | (sink == sequence[0]) | (lengths[sink] == 0), 0, jnp.maximum(slack, 0))
    passed = jax.random.randint(jax.random.fold_in(own, 4), (count // 2,), 0, 1 << 20) % (slack + 1)
    lengths = lengths.at[giver].add(-passed).at[sink].add(passed)
    items = jnp.searchsorted(jnp.cumsum(lengths), jnp.arange(rows * top), side="right").astype(jnp.int32)
    grid = items.reshape(top, rows).T
    grid = grid[jax.random.permutation(jax.random.fold_in(own, 1), rows)]
    turn = jax.random.randint(jax.random.fold_in(own, 2), (rows, 1), 0, top)
    return jnp.take_along_axis(grid, (jnp.arange(top)[None, :] + turn) % top, axis=1)


def load_shares(number_of, total, most, skew, full):
    weights = [(1 << 20) // math.isqrt(grade ** skew) + 1 for grade in range(1, number_of + 1)]
    largest = most if full else min(most, max(-(-total // number_of), total * weights[0] // sum(weights)))
    least = 1 if total - largest >= number_of - 1 else 0
    counts, spare = [largest] + [least] * (number_of - 1), total - largest - least * (number_of - 1)
    while spare > 0:
        candidates = [i for i in range(1, number_of) if counts[i] < largest] or [i for i in range(1, number_of) if counts[i] < most]
        whole, budget = sum([weights[i] for i in candidates]), spare
        for i in candidates:
            more = min(most - counts[i], max(1, budget * weights[i] // whole), spare)
            counts[i] = counts[i] + more
            spare = spare - more
    return np.array(counts)


def bell_draw(own_key, shape, width, limit, pieces=(), held_as=jnp.bfloat16):
    result = width * jax.random.normal(own_key, shape, jnp.float32)
    if pieces:
        result = result * steps_of(own_key, shape, pieces, -0.22, 0.18)
    return jnp.clip(result, -limit, limit).astype(held_as)


def setup_inputs(seed: int = 0) -> dict:
    key_of = jax.random.split(jax.random.key(seed), 15)
    query = bell_draw(key_of[0], (PACKED_SEQUENCES, PACKED_LENGTH, QUERY_HEADS * HEAD_WIDTH), 1.0, 6.0, ((0, 4), (1, 2), (2, 4)))
    keys = bell_draw(key_of[1], (PACKED_SEQUENCES, PACKED_LENGTH, KEY_VALUE_HEADS * HEAD_WIDTH), 1.0, 6.0, ((0, 4), (1, 2), (2, 4)))
    values = bell_draw(key_of[2], (PACKED_SEQUENCES, PACKED_LENGTH, KEY_VALUE_HEADS * HEAD_WIDTH), 4.0, 24.0, ((0, 4), (1, 2), (2, 4)))
    segment_ids = jax.vmap(lambda own: jnp.searchsorted(jnp.cumsum(uneven(own, 4, PACKED_LENGTH, PACKED_LENGTH // 2, 1)), jnp.arange(PACKED_LENGTH), side="right"))(jax.random.split(key_of[3], PACKED_SEQUENCES)).reshape((PACKED_SEQUENCES, PACKED_LENGTH)).astype(jnp.int32)
    query_norm_gain = jnp.clip(1.0 + 0.15 * jax.random.normal(key_of[4], (HEAD_WIDTH,), jnp.float32), 0.25, 1.75)
    key_norm_gain = jnp.clip(1.0 + 0.15 * jax.random.normal(key_of[5], (HEAD_WIDTH,), jnp.float32), 0.25, 1.75)
    out_weight = bell_draw(key_of[6], (QUERY_HEADS * HEAD_WIDTH, D), (QUERY_HEADS * HEAD_WIDTH) ** -0.5, 0.09375, ((0, 4), (1, 2)))
    residual = bell_draw(key_of[7], (PACKED_SEQUENCES, PACKED_LENGTH, D), 0.5, 3.0, ((0, 4), (1, 2)))
    norm_gain = jnp.clip(1.0 + 0.15 * jax.random.normal(key_of[8], (D,), jnp.float32), 0.25, 1.75)
    router_weight = bell_draw(key_of[9], (D, EXPERTS), D ** -0.5, 0.125)
    expert_ids_keys = jax.random.split(jax.random.fold_in(key_of[10], 1), PACKED_SEQUENCES * PACKED_LENGTH // MOE_DEV)
    expert_ids_turns = jax.random.permutation(jax.random.fold_in(key_of[10], 3), PACKED_SEQUENCES * PACKED_LENGTH // MOE_DEV)
    expert_ids = jax.vmap(lambda own, number: shared_out(jax.random.fold_in(key_of[10], 2), own, number, MOE_DEV, EXPERTS, TOP, CAP, 1))(expert_ids_keys, expert_ids_turns).reshape((PACKED_SEQUENCES, PACKED_LENGTH, TOP))
    expert_gate = bell_draw(key_of[11], (EXPERTS, D, FF), D ** -0.5, 0.125, ((0, 16), (2, 2)))
    expert_up = bell_draw(key_of[12], (EXPERTS, D, FF), D ** -0.5, 0.125, ((0, 16), (2, 2)))
    expert_down = bell_draw(key_of[13], (EXPERTS, D, FF), FF ** -0.5, 0.21875, ((0, 16), (2, 2)))
    return dict(query=query, keys=keys, values=values, segment_ids=segment_ids, query_norm_gain=query_norm_gain, key_norm_gain=key_norm_gain, out_weight=out_weight, residual=residual, norm_gain=norm_gain, router_weight=router_weight, expert_ids=expert_ids, expert_gate=expert_gate, expert_up=expert_up, expert_down=expert_down)


def root_mean_scale(entries, gain):
    mean_sq = lax.optimization_barrier(jnp.mean(entries * entries, axis=-1, keepdims=True))
    return entries * lax.rsqrt(mean_sq + 1e-06) * gain

def reference(query, keys, values, segment_ids, query_norm_gain, key_norm_gain, out_weight, residual, norm_gain, router_weight, expert_ids, expert_gate, expert_up, expert_down):
    query_group = QUERY_HEADS // KEY_VALUE_HEADS
    score_scale = HEAD_WIDTH ** (-0.5)

    def per_sequence(items):
        query_row, key_row, value_row, s_row, r_row, id_row = items
        query_rows_normed = root_mean_scale(query_row.astype(jnp.float32).reshape(PACKED_LENGTH, KEY_VALUE_HEADS, query_group, HEAD_WIDTH), query_norm_gain).astype(jnp.bfloat16)
        key_rows_normed = root_mean_scale(key_row.astype(jnp.float32).reshape(PACKED_LENGTH, KEY_VALUE_HEADS, HEAD_WIDTH), key_norm_gain).astype(jnp.bfloat16)
        value_heads = value_row.reshape(PACKED_LENGTH, KEY_VALUE_HEADS, HEAD_WIDTH)
        scores = jnp.einsum('lkgd,mkd->kglm', query_rows_normed.astype(jnp.float32), key_rows_normed.astype(jnp.float32)) * score_scale
        same_doc = s_row[:, None] == s_row[None, :]
        probs = jnp.where(same_doc[None, None], jnp.exp(scores), jnp.float32(0.0))
        denom = lax.optimization_barrier(jnp.sum(probs, axis=-1))
        probs_b = probs.astype(jnp.bfloat16)
        summed = jnp.einsum('kglm,mkd->lkgd', probs_b.astype(jnp.float32), value_heads.astype(jnp.float32))
        attn = (summed / jnp.transpose(denom, (2, 0, 1))[..., None]).astype(jnp.bfloat16).reshape(PACKED_LENGTH, QUERY_HEADS * HEAD_WIDTH)
        projected = jnp.dot(attn, out_weight, preferred_element_type=jnp.float32)
        state = r_row.astype(jnp.float32) + projected
        normed = root_mean_scale(state, norm_gain).astype(jnp.bfloat16)
        logits = jnp.dot(normed, router_weight, preferred_element_type=jnp.float32)
        chosen = jnp.take_along_axis(logits, id_row, axis=1)
        raised = jnp.exp(chosen)
        gates = raised / lax.optimization_barrier(jnp.sum(raised, axis=-1, keepdims=True))
        return (state, normed, gates)
    state, normed, gates = lax.map(per_sequence, (query, keys, values, segment_ids, residual, expert_ids))
    tokens = PACKED_SEQUENCES * PACKED_LENGTH
    flat_normed = normed.reshape(tokens, D)
    flat_ids = expert_ids.reshape(tokens * TOP)
    flat_gates = gates.reshape(tokens * TOP)
    bound = tokens // MOE_DEV * CAP

    def per_expert(mixture, expert):
        order = jnp.argsort((flat_ids != expert).astype(jnp.int32), stable=True)[:bound].astype(jnp.int32)
        live = flat_ids[order] == expert
        token = order // TOP
        picked_rows = flat_normed[token]
        gate_mat = lax.dynamic_index_in_dim(expert_gate, expert, 0, keepdims=False)
        up_mat = lax.dynamic_index_in_dim(expert_up, expert, 0, keepdims=False)
        down_mat = lax.dynamic_index_in_dim(expert_down, expert, 0, keepdims=False)
        gate_act = jnp.dot(picked_rows, gate_mat, preferred_element_type=jnp.float32)
        up_act = jnp.dot(picked_rows, up_mat, preferred_element_type=jnp.float32)
        hidden_act = (jax.nn.silu(gate_act) * up_act).astype(jnp.bfloat16)
        expert_out = jnp.einsum('rf,df->rd', hidden_act.astype(jnp.float32), down_mat.astype(jnp.float32)).astype(jnp.bfloat16)
        weight = jnp.where(live, flat_gates[order], jnp.float32(0.0))
        mixture = mixture.at[token].add(weight[:, None] * expert_out.astype(jnp.float32))
        return (mixture, None)
    mixture, _ = lax.scan(per_expert, jnp.zeros((tokens, D), jnp.float32), jnp.arange(EXPERTS, dtype=jnp.int32))
    layer_out = (state.reshape(tokens, D) + mixture).astype(jnp.bfloat16)
    return layer_out.reshape(PACKED_SEQUENCES, PACKED_LENGTH, D)
```

```python
import functools

import jax
import jax.numpy as jnp
from jax import lax
from jax.sharding import PartitionSpec as P

HEAD_WIDTH = 128


def root_mean_scale(entries, gain):
    mean_sq = jnp.mean(entries * entries, axis=-1, keepdims=True)
    return entries * lax.rsqrt(mean_sq + 1e-06) * gain


def capacity(share, top_count, experts):
    return min(
        share, max(2, share * top_count // experts + max(1, share * top_count // (8 * experts)))
    )


def slot_numbers(ids, experts):
    flat_ids = ids.reshape(-1)
    table = (flat_ids[:, None] == jnp.arange(experts, dtype=jnp.int32)[None, :]).astype(jnp.int32)
    before = jnp.cumsum(table, axis=0) - table
    return jnp.sum(before * table, axis=1).reshape(ids.shape)


def route(state, ids, norm_gain, router_weight):
    normed = root_mean_scale(state, norm_gain).astype(jnp.bfloat16)
    logits = jnp.dot(normed, router_weight, preferred_element_type=jnp.float32)
    experts = router_weight.shape[1]
    picks = ids[:, :, None] == jnp.arange(experts, dtype=jnp.int32)[None, None, :]
    chosen = jnp.sum(jnp.where(picks, logits[:, None, :], jnp.float32(0.0)), axis=-1)
    raised = jnp.exp(chosen)
    return (normed, raised / jnp.sum(raised, axis=-1, keepdims=True))


def cp_pieces(x, n_cp):
    pieces = [x]
    for shift in range(1, n_cp):
        perm = [(i, (i + shift) % n_cp) for i in range(n_cp)]
        pieces.append(lax.ppermute(x, "cp", perm))
    return pieces


def expert_rows(received, full_gate, full_up, full_down):
    width = received.shape[-1]
    flat_rows = received.reshape(-1, width)
    gate_act = jnp.dot(flat_rows, full_gate[0], preferred_element_type=jnp.float32)
    up_act = jnp.dot(flat_rows, full_up[0], preferred_element_type=jnp.float32)
    hidden_act = (jax.nn.silu(gate_act) * up_act).astype(jnp.bfloat16)
    served = jnp.einsum(
        "rf,df->rd", hidden_act, full_down[0], preferred_element_type=jnp.float32
    ).astype(jnp.bfloat16)
    return served.reshape(received.shape)


def shards(
    query,
    keys,
    values,
    segment_ids,
    query_norm_gain,
    key_norm_gain,
    out_weight,
    residual,
    norm_gain,
    router_weight,
    expert_ids,
    expert_gate,
    expert_up,
    expert_down,
    *,
    n_cp,
    n_tp,
    n_ep,
):
    packs = query.shape[0]
    row_count = query.shape[1]
    head_count = query.shape[2] // HEAD_WIDTH
    width = residual.shape[2]
    experts = router_weight.shape[1]
    top_count = expert_ids.shape[2]
    score_scale = HEAD_WIDTH ** (-0.5)

    query_rows_normed = root_mean_scale(
        query.astype(jnp.float32).reshape(packs, row_count, head_count, HEAD_WIDTH), query_norm_gain
    ).astype(jnp.bfloat16)
    key_rows_normed = root_mean_scale(keys.astype(jnp.float32), key_norm_gain).astype(jnp.bfloat16)
    key_value = jnp.concatenate([key_rows_normed, values], axis=-1)
    kv_all = jnp.concatenate(cp_pieces(key_value, n_cp), axis=1)
    doc_all = jnp.concatenate(cp_pieces(segment_ids, n_cp), axis=1)
    key_piece = kv_all[..., :HEAD_WIDTH]
    value_piece = kv_all[..., HEAD_WIDTH:]
    scores = (
        jnp.einsum(
            "pshd,pnd->phsn", query_rows_normed, key_piece, preferred_element_type=jnp.float32
        )
        * score_scale
    )
    same_doc = segment_ids[:, :, None] == doc_all[:, None, :]
    probs = jnp.where(same_doc[:, None], jnp.exp(scores), jnp.float32(0.0))
    denom = jnp.sum(probs, axis=-1)
    probs_b = probs.astype(jnp.bfloat16)
    summed = jnp.einsum("phsn,pnd->pshd", probs_b, value_piece, preferred_element_type=jnp.float32)
    attn = (
        (summed / jnp.transpose(denom, (0, 2, 1))[:, :, :, None])
        .astype(jnp.bfloat16)
        .reshape(packs * row_count, head_count * HEAD_WIDTH)
    )
    full_out_weight = lax.all_gather(out_weight, "cp", axis=1, tiled=True)
    partial_proj = jnp.dot(
        attn, full_out_weight, preferred_element_type=jnp.float32
    ).reshape(packs, row_count, width)

    full_out_weight, expert_gate, expert_up, expert_down = lax.optimization_barrier(
        (full_out_weight, expert_gate, expert_up, expert_down)
    )
    full_gate = jnp.concatenate(cp_pieces(expert_gate, n_cp), axis=2)
    full_up = jnp.concatenate(cp_pieces(expert_up, n_cp), axis=2)
    full_down = jnp.concatenate(cp_pieces(expert_down, n_cp), axis=2)

    share = row_count // n_tp
    tp_index = lax.axis_index("tp")
    ep_index = lax.axis_index("ep")
    cap = capacity(share, top_count, experts)
    projected = lax.psum_scatter(partial_proj, "tp", scatter_dimension=1, tiled=True)
    first_row = tp_index * share
    state = lax.dynamic_slice_in_dim(residual, first_row, share, 1).astype(jnp.float32) + projected
    local_ids = lax.dynamic_slice_in_dim(expert_ids, first_row, share, 1).reshape(
        packs * share, top_count
    )
    normed, gates = route(state.reshape(packs * share, width), local_ids, norm_gain, router_weight)
    dev_cap = packs * cap
    slots = slot_numbers(local_ids, experts)

    home_rows = packs * share
    meta = jnp.concatenate(
        [local_ids.astype(jnp.float32), slots.astype(jnp.float32), gates], axis=-1
    )
    normed_all = lax.all_gather(normed, "ep", axis=0, tiled=True)
    meta_all = lax.all_gather(meta, "ep", axis=0, tiled=True)
    ids_all = meta_all[:, :top_count].astype(jnp.int32)
    slots_all = meta_all[:, top_count : 2 * top_count].astype(jnp.int32)
    gates_all = meta_all[:, 2 * top_count :]
    gathered = n_ep * home_rows
    home_of = (jnp.arange(gathered, dtype=jnp.int32) // home_rows)[:, None]
    cap2 = n_ep * dev_cap
    n_slots = n_tp * cap2
    mine = (ids_all % n_ep) == ep_index
    target = jnp.where(
        mine, (ids_all // n_ep) * cap2 + home_of * dev_cap + slots_all, jnp.int32(-1)
    )
    hit = target[None, :, :] == jnp.arange(n_slots, dtype=jnp.int32)[:, None, None]
    select = jnp.any(hit, axis=-1).astype(jnp.bfloat16)
    weight = jnp.sum(jnp.where(hit, gates_all[None, :, :], jnp.float32(0.0)), axis=-1)

    buffer = jnp.dot(select, normed_all, preferred_element_type=jnp.float32).astype(jnp.bfloat16)
    received = lax.all_to_all(
        buffer.reshape(n_tp, cap2, width), "tp", split_axis=0, concat_axis=0, tiled=True
    )
    served = expert_rows(received, full_gate, full_up, full_down)
    back = lax.all_to_all(served, "tp", split_axis=0, concat_axis=0, tiled=True).reshape(
        n_slots, width
    )

    weight_hi = weight.astype(jnp.bfloat16)
    weight_lo = (weight - weight_hi.astype(jnp.float32)).astype(jnp.bfloat16)
    contract = (((0,), (0,)), ((), ()))
    partial = lax.dot_general(
        weight_hi, back, contract, preferred_element_type=jnp.float32
    ) + lax.dot_general(weight_lo, back, contract, preferred_element_type=jnp.float32)
    mixture = lax.psum_scatter(
        partial.reshape(n_ep, home_rows, width), "ep", scatter_dimension=0, tiled=True
    )
    layer_out = (state + mixture.reshape(packs, share, width)).astype(jnp.bfloat16)
    return layer_out


def solution(mesh):
    body = functools.partial(
        shards, n_cp=mesh.shape["cp"], n_tp=mesh.shape["tp"], n_ep=mesh.shape["ep"]
    )
    return jax.shard_map(
        body,
        mesh=mesh,
        in_specs=(
            P("ep", "cp", "tp"),
            P("ep", "cp", "tp"),
            P("ep", "cp", "tp"),
            P("ep", "cp"),
            P(),
            P(),
            P("tp", "cp"),
            P("ep", "cp", None),
            P(),
            P(),
            P("ep", "cp", None),
            P(("tp", "ep"), None, "cp"),
            P(("tp", "ep"), None, "cp"),
            P(("tp", "ep"), None, "cp"),
        ),
        out_specs=P("ep", ("cp", "tp"), None),
        check_vma=False,
    )
```

```python
import functools

import jax
import jax.numpy as jnp
from jax import lax
from jax.sharding import PartitionSpec as P

HEAD_WIDTH = 128


def root_mean_scale(entries, gain):
    mean_sq = jnp.mean(entries * entries, axis=-1, keepdims=True)
    return entries * lax.rsqrt(mean_sq + 1e-06) * gain


def capacity(share, top_count, experts):
    return min(
        share, max(2, share * top_count // experts + max(1, share * top_count // (8 * experts)))
    )


def slot_numbers(ids, experts):
    flat_ids = ids.reshape(-1)
    table = (flat_ids[:, None] == jnp.arange(experts, dtype=jnp.int32)[None, :]).astype(jnp.int32)
    before = jnp.cumsum(table, axis=0) - table
    return jnp.sum(before * table, axis=1).reshape(ids.shape)


def route(state, ids, norm_gain, router_weight):
    normed = root_mean_scale(state, norm_gain).astype(jnp.bfloat16)
    logits = jnp.dot(normed, router_weight, preferred_element_type=jnp.float32)
    experts = router_weight.shape[1]
    picks = ids[:, :, None] == jnp.arange(experts, dtype=jnp.int32)[None, None, :]
    chosen = jnp.sum(jnp.where(picks, logits[:, None, :], jnp.float32(0.0)), axis=-1)
    raised = jnp.exp(chosen)
    return (normed, raised / jnp.sum(raised, axis=-1, keepdims=True))


def cp_pieces(x, n_cp):
    pieces = [x]
    for shift in range(1, n_cp):
        perm = [(i, (i + shift) % n_cp) for i in range(n_cp)]
        pieces.append(lax.ppermute(x, "cp", perm))
    return pieces


def expert_rows(received, full_gate, full_up, full_down):
    width = received.shape[-1]
    flat_rows = received.reshape(-1, width)
    gate_act = jnp.dot(flat_rows, full_gate[0], preferred_element_type=jnp.float32)
    up_act = jnp.dot(flat_rows, full_up[0], preferred_element_type=jnp.float32)
    hidden_act = (jax.nn.silu(gate_act) * up_act).astype(jnp.bfloat16)
    served = jnp.einsum(
        "rf,df->rd", hidden_act, full_down[0], preferred_element_type=jnp.float32
    ).astype(jnp.bfloat16)
    return served.reshape(received.shape)


def shards(
    query,
    keys,
    values,
    segment_ids,
    query_norm_gain,
    key_norm_gain,
    out_weight,
    residual,
    norm_gain,
    router_weight,
    expert_ids,
    expert_gate,
    expert_up,
    expert_down,
    *,
    n_cp,
    n_tp,
    n_ep,
):
    packs = query.shape[0]
    row_count = query.shape[1]
    head_count = query.shape[2] // HEAD_WIDTH
    width = residual.shape[2]
    experts = router_weight.shape[1]
    top_count = expert_ids.shape[2]
    score_scale = HEAD_WIDTH ** (-0.5)

    query_rows_normed = root_mean_scale(
        query.astype(jnp.float32).reshape(packs, row_count, head_count, HEAD_WIDTH), query_norm_gain
    ).astype(jnp.bfloat16)
    key_rows_normed = root_mean_scale(keys.astype(jnp.float32), key_norm_gain).astype(jnp.bfloat16)
    key_value = jnp.concatenate([key_rows_normed, values], axis=-1)
    kv_all = jnp.concatenate(cp_pieces(key_value, n_cp), axis=1)
    doc_all = jnp.concatenate(cp_pieces(segment_ids, n_cp), axis=1)
    key_piece = kv_all[..., :HEAD_WIDTH]
    value_piece = kv_all[..., HEAD_WIDTH:]
    scores = (
        jnp.einsum(
            "pshd,pnd->phsn", query_rows_normed, key_piece, preferred_element_type=jnp.float32
        )
        * score_scale
    )
    same_doc = segment_ids[:, :, None] == doc_all[:, None, :]
    probs = jnp.where(same_doc[:, None], jnp.exp(scores), jnp.float32(0.0))
    denom = jnp.sum(probs, axis=-1)
    probs_b = probs.astype(jnp.bfloat16)
    summed = jnp.einsum("phsn,pnd->pshd", probs_b, value_piece, preferred_element_type=jnp.float32)
    attn = (
        (summed / jnp.transpose(denom, (0, 2, 1))[:, :, :, None])
        .astype(jnp.bfloat16)
        .reshape(packs * row_count, head_count * HEAD_WIDTH)
    )
    full_out_weight = lax.all_gather(out_weight, "cp", axis=1, tiled=True)
    partial_proj = jnp.dot(
        attn, full_out_weight, preferred_element_type=jnp.float32
    ).reshape(packs, row_count, width)

    share = row_count // n_tp
    tp_index = lax.axis_index("tp")
    ep_index = lax.axis_index("ep")
    cap = capacity(share, top_count, experts)
    projected = lax.psum_scatter(partial_proj, "tp", scatter_dimension=1, tiled=True)
    first_row = tp_index * share
    state = lax.dynamic_slice_in_dim(residual, first_row, share, 1).astype(jnp.float32) + projected
    local_ids = lax.dynamic_slice_in_dim(expert_ids, first_row, share, 1).reshape(
        packs * share, top_count
    )
    home_rows = packs * share
    normed = root_mean_scale(state.reshape(home_rows, width), norm_gain).astype(jnp.bfloat16)

    full_out_weight, expert_gate, expert_up, expert_down = lax.optimization_barrier(
        (full_out_weight, expert_gate, expert_up, expert_down)
    )
    gate_pieces = cp_pieces(expert_gate, n_cp)
    up_pieces = cp_pieces(expert_up, n_cp)
    down_pieces = cp_pieces(expert_down, n_cp)
    normed, gate_pieces, up_pieces = lax.optimization_barrier((normed, gate_pieces, up_pieces))

    lanes = 128
    id_lanes = jnp.pad(local_ids.astype(jnp.bfloat16), ((0, 0), (0, lanes - top_count)))
    rows_all = lax.all_gather(
        jnp.concatenate([normed, id_lanes], axis=1), "ep", axis=0, tiled=True
    )
    normed_all = rows_all[:, :width]
    ids_all = rows_all[:, width : width + top_count].astype(jnp.int32)
    logits = jnp.dot(normed_all, router_weight, preferred_element_type=jnp.float32)
    picks = ids_all[:, :, None] == jnp.arange(experts, dtype=jnp.int32)[None, None, :]
    raised = jnp.exp(jnp.sum(jnp.where(picks, logits[:, None, :], jnp.float32(0.0)), axis=-1))
    gates_all = raised / jnp.sum(raised, axis=-1, keepdims=True)

    gathered = n_ep * home_rows
    dev_cap = packs * cap
    cap2 = n_ep * dev_cap
    n_slots = n_tp * cap2
    mine = (ids_all % n_ep) == ep_index
    dest = ids_all // n_ep
    named = jnp.stack(
        [jnp.any(mine & (dest == j), axis=1) for j in range(n_tp)], axis=1
    ).astype(jnp.bfloat16)
    row_iota = jnp.arange(gathered, dtype=jnp.int32)
    earlier = (row_iota[:, None] > row_iota[None, :]).astype(jnp.bfloat16)
    rank = jnp.dot(earlier, named, preferred_element_type=jnp.float32).astype(jnp.int32)
    rank_of = jnp.sum(
        jnp.where(dest[:, :, None] == jnp.arange(n_tp, dtype=jnp.int32)[None, None, :],
                  rank[:, None, :], 0),
        axis=-1,
    )
    target = jnp.where(mine, dest * cap2 + rank_of, jnp.int32(-1)).T
    hit = target[:, None, :] == jnp.arange(n_slots, dtype=jnp.int32)[None, :, None]
    select = jnp.any(hit, axis=0).astype(jnp.bfloat16)
    weight = jnp.sum(jnp.where(hit, gates_all.T[:, None, :], jnp.float32(0.0)), axis=0)

    buffer = jnp.dot(select, normed_all, preferred_element_type=jnp.float32).astype(jnp.bfloat16)
    buffer, down_pieces = lax.optimization_barrier((buffer, down_pieces))
    full_gate = jnp.concatenate(gate_pieces, axis=2)
    full_up = jnp.concatenate(up_pieces, axis=2)
    full_down = jnp.concatenate(down_pieces, axis=2)
    received = lax.all_to_all(
        buffer.reshape(n_tp, cap2, width), "tp", split_axis=0, concat_axis=0, tiled=True
    )
    served = expert_rows(received, full_gate, full_up, full_down)
    back = lax.all_to_all(served, "tp", split_axis=0, concat_axis=0, tiled=True).reshape(
        n_slots, width
    )

    weight_hi = weight.astype(jnp.bfloat16)
    weight_lo = (weight - weight_hi.astype(jnp.float32)).astype(jnp.bfloat16)
    contract = (((0,), (0,)), ((), ()))
    partial = lax.dot_general(
        weight_hi, back, contract, preferred_element_type=jnp.float32
    ) + lax.dot_general(weight_lo, back, contract, preferred_element_type=jnp.float32)
    mixture = lax.psum_scatter(
        partial.astype(jnp.bfloat16).reshape(n_ep, home_rows, width),
        "ep",
        scatter_dimension=0,
        tiled=True,
    )
    layer_out = (state + mixture.astype(jnp.float32).reshape(packs, share, width)).astype(
        jnp.bfloat16
    )
    return layer_out


def solution(mesh):
    body = functools.partial(
        shards, n_cp=mesh.shape["cp"], n_tp=mesh.shape["tp"], n_ep=mesh.shape["ep"]
    )
    return jax.shard_map(
        body,
        mesh=mesh,
        in_specs=(
            P("ep", "cp", "tp"),
            P("ep", "cp", "tp"),
            P("ep", "cp", "tp"),
            P("ep", "cp"),
            P(),
            P(),
            P("tp", "cp"),
            P("ep", "cp", None),
            P(),
            P(),
            P("ep", "cp", None),
            P(("tp", "ep"), None, "cp"),
            P(("tp", "ep"), None, "cp"),
            P(("tp", "ep"), None, "cp"),
        ),
        out_specs=P("ep", ("cp", "tp"), None),
        check_vma=False,
    )
```

```python
import functools

import jax
import jax.numpy as jnp
from jax import lax
from jax.sharding import PartitionSpec as P

HEAD_WIDTH = 128


def root_mean_scale(entries, gain):
    mean_sq = jnp.mean(entries * entries, axis=-1, keepdims=True)
    return entries * lax.rsqrt(mean_sq + 1e-06) * gain


def capacity(share, top_count, experts):
    return min(
        share, max(2, share * top_count // experts + max(1, share * top_count // (8 * experts)))
    )


def slot_numbers(ids, experts):
    flat_ids = ids.reshape(-1)
    table = (flat_ids[:, None] == jnp.arange(experts, dtype=jnp.int32)[None, :]).astype(jnp.int32)
    before = jnp.cumsum(table, axis=0) - table
    return jnp.sum(before * table, axis=1).reshape(ids.shape)


def route(state, ids, norm_gain, router_weight):
    normed = root_mean_scale(state, norm_gain).astype(jnp.bfloat16)
    logits = jnp.dot(normed, router_weight, preferred_element_type=jnp.float32)
    experts = router_weight.shape[1]
    picks = ids[:, :, None] == jnp.arange(experts, dtype=jnp.int32)[None, None, :]
    chosen = jnp.sum(jnp.where(picks, logits[:, None, :], jnp.float32(0.0)), axis=-1)
    raised = jnp.exp(chosen)
    return (normed, raised / jnp.sum(raised, axis=-1, keepdims=True))


def cp_pieces(x, n_cp):
    pieces = [x]
    for shift in range(1, n_cp):
        perm = [(i, (i + shift) % n_cp) for i in range(n_cp)]
        pieces.append(lax.ppermute(x, "cp", perm))
    return pieces


def expert_rows(received, full_gate, full_up, full_down):
    width = received.shape[-1]
    flat_rows = received.reshape(-1, width)
    gate_act = jnp.dot(flat_rows, full_gate[0], preferred_element_type=jnp.float32)
    up_act = jnp.dot(flat_rows, full_up[0], preferred_element_type=jnp.float32)
    hidden_act = (jax.nn.silu(gate_act) * up_act).astype(jnp.bfloat16)
    served = jnp.einsum(
        "rf,df->rd", hidden_act, full_down[0], preferred_element_type=jnp.float32
    ).astype(jnp.bfloat16)
    return served.reshape(received.shape)


def shards(
    query,
    keys,
    values,
    segment_ids,
    query_norm_gain,
    key_norm_gain,
    out_weight,
    residual,
    norm_gain,
    router_weight,
    expert_ids,
    expert_gate,
    expert_up,
    expert_down,
    *,
    n_cp,
    n_tp,
    n_ep,
):
    packs = query.shape[0]
    row_count = query.shape[1]
    head_count = query.shape[2] // HEAD_WIDTH
    width = residual.shape[2]
    experts = router_weight.shape[1]
    top_count = expert_ids.shape[2]
    score_scale = HEAD_WIDTH ** (-0.5)

    query_rows_normed = root_mean_scale(
        query.astype(jnp.float32).reshape(packs, row_count, head_count, HEAD_WIDTH), query_norm_gain
    ).astype(jnp.bfloat16)
    key_rows_normed = root_mean_scale(keys.astype(jnp.float32), key_norm_gain).astype(jnp.bfloat16)
    key_value = jnp.concatenate([key_rows_normed, values], axis=-1)
    kv_all = jnp.concatenate(cp_pieces(key_value, n_cp), axis=1)
    doc_all = jnp.concatenate(cp_pieces(segment_ids, n_cp), axis=1)
    key_piece = kv_all[..., :HEAD_WIDTH]
    value_piece = kv_all[..., HEAD_WIDTH:]
    scores = (
        jnp.einsum(
            "pshd,pnd->phsn", query_rows_normed, key_piece, preferred_element_type=jnp.float32
        )
        * score_scale
    )
    same_doc = segment_ids[:, :, None] == doc_all[:, None, :]
    probs = jnp.where(same_doc[:, None], jnp.exp(scores), jnp.float32(0.0))
    denom = jnp.sum(probs, axis=-1)
    probs_b = probs.astype(jnp.bfloat16)
    summed = jnp.einsum("phsn,pnd->pshd", probs_b, value_piece, preferred_element_type=jnp.float32)
    attn = (
        (summed / jnp.transpose(denom, (0, 2, 1))[:, :, :, None])
        .astype(jnp.bfloat16)
        .reshape(packs * row_count, head_count * HEAD_WIDTH)
    )
    full_out_weight = jnp.concatenate(cp_pieces(out_weight, n_cp), axis=1)
    partial_proj = jnp.dot(
        attn, full_out_weight, preferred_element_type=jnp.float32
    ).reshape(packs, row_count, width)

    share = row_count // n_tp
    tp_index = lax.axis_index("tp")
    ep_index = lax.axis_index("ep")
    cap = capacity(share, top_count, experts)
    projected = lax.psum_scatter(
        partial_proj.astype(jnp.bfloat16), "tp", scatter_dimension=1, tiled=True
    ).astype(jnp.float32)
    cp_index = lax.axis_index("cp")
    block_width = width // n_cp
    blocks = projected.reshape(packs, share, n_cp, block_width)
    source_block = (cp_index - jnp.arange(n_cp, dtype=jnp.int32)) % n_cp
    picks_block = source_block[:, None] == jnp.arange(n_cp, dtype=jnp.int32)[None, :]
    projected = jnp.sum(
        jnp.where(picks_block[None, None, :, :, None], blocks[:, :, None, :, :], jnp.float32(0.0)),
        axis=3,
    ).reshape(packs, share, width)
    first_row = tp_index * share
    state = lax.dynamic_slice_in_dim(residual, first_row, share, 1).astype(jnp.float32) + projected
    local_ids = lax.dynamic_slice_in_dim(expert_ids, first_row, share, 1).reshape(
        packs * share, top_count
    )
    home_rows = packs * share
    normed = root_mean_scale(state.reshape(home_rows, width), norm_gain).astype(jnp.bfloat16)

    full_out_weight, expert_gate, expert_up, expert_down = lax.optimization_barrier(
        (full_out_weight, expert_gate, expert_up, expert_down)
    )
    gate_pieces = cp_pieces(expert_gate, n_cp)
    up_pieces = cp_pieces(expert_up, n_cp)
    down_pieces = cp_pieces(expert_down, n_cp)
    normed, gate_pieces, up_pieces = lax.optimization_barrier((normed, gate_pieces, up_pieces))

    lanes = 128
    id_lanes = jnp.pad(local_ids.astype(jnp.bfloat16), ((0, 0), (0, lanes - top_count)))
    rows_all = lax.all_gather(
        jnp.concatenate([normed, id_lanes], axis=1), "ep", axis=0, tiled=True
    )
    normed_all = rows_all[:, :width]
    ids_all = rows_all[:, width : width + top_count].astype(jnp.int32)
    logits = jnp.dot(normed_all, router_weight, preferred_element_type=jnp.float32)
    picks = ids_all[:, :, None] == jnp.arange(experts, dtype=jnp.int32)[None, None, :]
    raised = jnp.exp(jnp.sum(jnp.where(picks, logits[:, None, :], jnp.float32(0.0)), axis=-1))
    gates_all = raised / jnp.sum(raised, axis=-1, keepdims=True)

    gathered = n_ep * home_rows
    dev_cap = packs * cap
    cap2 = n_ep * dev_cap
    n_slots = n_tp * cap2
    mine = (ids_all % n_ep) == ep_index
    dest = ids_all // n_ep
    named = jnp.stack(
        [jnp.any(mine & (dest == j), axis=1) for j in range(n_tp)], axis=1
    ).astype(jnp.bfloat16)
    row_iota = jnp.arange(gathered, dtype=jnp.int32)
    earlier = (row_iota[:, None] > row_iota[None, :]).astype(jnp.bfloat16)
    rank = jnp.dot(earlier, named, preferred_element_type=jnp.float32).astype(jnp.int32)
    rank_of = jnp.sum(
        jnp.where(dest[:, :, None] == jnp.arange(n_tp, dtype=jnp.int32)[None, None, :],
                  rank[:, None, :], 0),
        axis=-1,
    )
    target = jnp.where(mine, dest * cap2 + rank_of, jnp.int32(-1)).T
    hit = target[:, None, :] == jnp.arange(n_slots, dtype=jnp.int32)[None, :, None]
    select = jnp.any(hit, axis=0).astype(jnp.bfloat16)
    weight = jnp.sum(jnp.where(hit, gates_all.T[:, None, :], jnp.float32(0.0)), axis=0)

    buffer = jnp.dot(select, normed_all, preferred_element_type=jnp.float32).astype(jnp.bfloat16)
    buffer, down_pieces = lax.optimization_barrier((buffer, down_pieces))
    full_gate = jnp.concatenate(gate_pieces, axis=2)
    full_up = jnp.concatenate(up_pieces, axis=2)
    full_down = jnp.concatenate(down_pieces, axis=2)
    received = lax.all_to_all(
        buffer.reshape(n_tp, cap2, width), "tp", split_axis=0, concat_axis=0, tiled=True
    )
    served = expert_rows(received, full_gate, full_up, full_down)
    back = lax.all_to_all(served, "tp", split_axis=0, concat_axis=0, tiled=True).reshape(
        n_slots, width
    )

    weight_hi = weight.astype(jnp.bfloat16)
    weight_lo = (weight - weight_hi.astype(jnp.float32)).astype(jnp.bfloat16)
    contract = (((0,), (0,)), ((), ()))
    partial = lax.dot_general(
        weight_hi, back, contract, preferred_element_type=jnp.float32
    ) + lax.dot_general(weight_lo, back, contract, preferred_element_type=jnp.float32)
    mixture = lax.psum_scatter(
        partial.astype(jnp.bfloat16).reshape(n_ep, home_rows, width),
        "ep",
        scatter_dimension=0,
        tiled=True,
    )
    layer_out = (state + mixture.astype(jnp.float32).reshape(packs, share, width)).astype(
        jnp.bfloat16
    )
    return layer_out


def solution(mesh):
    body = functools.partial(
        shards, n_cp=mesh.shape["cp"], n_tp=mesh.shape["tp"], n_ep=mesh.shape["ep"]
    )
    return jax.shard_map(
        body,
        mesh=mesh,
        in_specs=(
            P("ep", "cp", "tp"),
            P("ep", "cp", "tp"),
            P("ep", "cp", "tp"),
            P("ep", "cp"),
            P(),
            P(),
            P("tp", "cp"),
            P("ep", "cp", None),
            P(),
            P(),
            P("ep", "cp", None),
            P(("tp", "ep"), None, "cp"),
            P(("tp", "ep"), None, "cp"),
            P(("tp", "ep"), None, "cp"),
        ),
        out_specs=P("ep", ("cp", "tp"), None),
        check_vma=False,
    )
```

```python
import functools

import jax
import jax.numpy as jnp
from jax import lax
from jax.sharding import PartitionSpec as P

HEAD_WIDTH = 128


def root_mean_scale(entries, gain):
    mean_sq = jnp.mean(entries * entries, axis=-1, keepdims=True)
    return entries * lax.rsqrt(mean_sq + 1e-06) * gain


def capacity(share, top_count, experts):
    return min(
        share, max(2, share * top_count // experts + max(1, share * top_count // (8 * experts)))
    )


def slot_numbers(ids, experts):
    flat_ids = ids.reshape(-1)
    table = (flat_ids[:, None] == jnp.arange(experts, dtype=jnp.int32)[None, :]).astype(jnp.int32)
    before = jnp.cumsum(table, axis=0) - table
    return jnp.sum(before * table, axis=1).reshape(ids.shape)


def route(state, ids, norm_gain, router_weight):
    normed = root_mean_scale(state, norm_gain).astype(jnp.bfloat16)
    logits = jnp.dot(normed, router_weight, preferred_element_type=jnp.float32)
    experts = router_weight.shape[1]
    picks = ids[:, :, None] == jnp.arange(experts, dtype=jnp.int32)[None, None, :]
    chosen = jnp.sum(jnp.where(picks, logits[:, None, :], jnp.float32(0.0)), axis=-1)
    raised = jnp.exp(chosen)
    return (normed, raised / jnp.sum(raised, axis=-1, keepdims=True))


def cp_pieces(x, n_cp):
    pieces = [x]
    for shift in range(1, n_cp):
        perm = [(i, (i + shift) % n_cp) for i in range(n_cp)]
        pieces.append(lax.ppermute(x, "cp", perm))
    return pieces


def expert_rows(received, full_gate, full_up, full_down):
    width = received.shape[-1]
    flat_rows = received.reshape(-1, width)
    gate_act = jnp.dot(flat_rows, full_gate[0], preferred_element_type=jnp.float32)
    up_act = jnp.dot(flat_rows, full_up[0], preferred_element_type=jnp.float32)
    hidden_act = (jax.nn.silu(gate_act) * up_act).astype(jnp.bfloat16)
    served = jnp.einsum(
        "rf,df->rd", hidden_act, full_down[0], preferred_element_type=jnp.float32
    ).astype(jnp.bfloat16)
    return served.reshape(received.shape)


def shards(
    query,
    keys,
    values,
    segment_ids,
    query_norm_gain,
    key_norm_gain,
    out_weight,
    residual,
    norm_gain,
    router_weight,
    expert_ids,
    expert_gate,
    expert_up,
    expert_down,
    *,
    n_cp,
    n_tp,
    n_ep,
):
    packs = query.shape[0]
    row_count = query.shape[1]
    head_count = query.shape[2] // HEAD_WIDTH
    width = residual.shape[2]
    experts = router_weight.shape[1]
    top_count = expert_ids.shape[2]
    score_scale = HEAD_WIDTH ** (-0.5)

    query_rows_normed = root_mean_scale(
        query.astype(jnp.float32).reshape(packs, row_count, head_count, HEAD_WIDTH), query_norm_gain
    ).astype(jnp.bfloat16)
    key_rows_normed = root_mean_scale(keys.astype(jnp.float32), key_norm_gain).astype(jnp.bfloat16)
    key_value = jnp.concatenate([key_rows_normed, values], axis=-1)
    kv_all = jnp.concatenate(cp_pieces(key_value, n_cp), axis=1)
    doc_all = jnp.concatenate(cp_pieces(segment_ids, n_cp), axis=1)
    key_piece = kv_all[..., :HEAD_WIDTH]
    value_piece = kv_all[..., HEAD_WIDTH:]
    scores = (
        jnp.einsum(
            "pshd,pnd->phsn", query_rows_normed, key_piece, preferred_element_type=jnp.float32
        )
        * score_scale
    )
    same_doc = segment_ids[:, :, None] == doc_all[:, None, :]
    probs = jnp.where(same_doc[:, None], jnp.exp(scores), jnp.float32(0.0))
    denom = jnp.sum(probs, axis=-1)
    probs_b = probs.astype(jnp.bfloat16)
    summed = jnp.einsum("phsn,pnd->pshd", probs_b, value_piece, preferred_element_type=jnp.float32)
    attn = (
        (summed / jnp.transpose(denom, (0, 2, 1))[:, :, :, None])
        .astype(jnp.bfloat16)
        .reshape(packs * row_count, head_count * HEAD_WIDTH)
    )
    full_out_weight = jnp.concatenate(cp_pieces(out_weight, n_cp), axis=1)
    partial_proj = jnp.dot(
        attn, full_out_weight, preferred_element_type=jnp.float32
    ).reshape(packs, row_count, width)

    share = row_count // n_tp
    tp_index = lax.axis_index("tp")
    ep_index = lax.axis_index("ep")
    cap = capacity(share, top_count, experts)
    projected = lax.psum_scatter(
        partial_proj.astype(jnp.bfloat16), "tp", scatter_dimension=1, tiled=True
    ).astype(jnp.float32)
    cp_index = lax.axis_index("cp")
    block_width = width // n_cp
    blocks = projected.reshape(packs, share, n_cp, block_width)
    source_block = (cp_index - jnp.arange(n_cp, dtype=jnp.int32)) % n_cp
    picks_block = source_block[:, None] == jnp.arange(n_cp, dtype=jnp.int32)[None, :]
    projected = jnp.sum(
        jnp.where(picks_block[None, None, :, :, None], blocks[:, :, None, :, :], jnp.float32(0.0)),
        axis=3,
    ).reshape(packs, share, width)
    first_row = tp_index * share
    state = lax.dynamic_slice_in_dim(residual, first_row, share, 1).astype(jnp.float32) + projected
    local_ids = lax.dynamic_slice_in_dim(expert_ids, first_row, share, 1).reshape(
        packs * share, top_count
    )
    home_rows = packs * share
    normed = root_mean_scale(state.reshape(home_rows, width), norm_gain).astype(jnp.bfloat16)

    full_out_weight, expert_gate, expert_up, expert_down = lax.optimization_barrier(
        (full_out_weight, expert_gate, expert_up, expert_down)
    )
    gate_pieces = cp_pieces(expert_gate, n_cp)
    up_pieces = cp_pieces(expert_up, n_cp)
    down_pieces = cp_pieces(expert_down, n_cp)

    lanes = 128
    id_lanes = jnp.pad(local_ids.astype(jnp.bfloat16), ((0, 0), (0, lanes - top_count)))
    rows_all = lax.all_gather(
        jnp.concatenate([normed, id_lanes], axis=1), "ep", axis=0, tiled=True
    )
    normed_all = rows_all[:, :width]
    ids_all = rows_all[:, width : width + top_count].astype(jnp.int32)
    logits = jnp.dot(normed_all, router_weight, preferred_element_type=jnp.float32)
    picks = ids_all[:, :, None] == jnp.arange(experts, dtype=jnp.int32)[None, None, :]
    raised = jnp.exp(jnp.sum(jnp.where(picks, logits[:, None, :], jnp.float32(0.0)), axis=-1))
    gates_all = raised / jnp.sum(raised, axis=-1, keepdims=True)

    gathered = n_ep * home_rows
    dev_cap = packs * cap
    cap2 = n_ep * dev_cap
    n_slots = n_tp * cap2
    mine = (ids_all % n_ep) == ep_index
    dest = ids_all // n_ep
    named = jnp.stack(
        [jnp.any(mine & (dest == j), axis=1) for j in range(n_tp)], axis=1
    ).astype(jnp.bfloat16)
    row_iota = jnp.arange(gathered, dtype=jnp.int32)
    earlier = (row_iota[:, None] > row_iota[None, :]).astype(jnp.bfloat16)
    rank = jnp.dot(earlier, named, preferred_element_type=jnp.float32).astype(jnp.int32)
    rank_of = jnp.sum(
        jnp.where(dest[:, :, None] == jnp.arange(n_tp, dtype=jnp.int32)[None, None, :],
                  rank[:, None, :], 0),
        axis=-1,
    )
    target = jnp.where(mine, dest * cap2 + rank_of, jnp.int32(-1)).T
    target, gate_pieces, up_pieces = lax.optimization_barrier((target, gate_pieces, up_pieces))
    hit = target[:, None, :] == jnp.arange(n_slots, dtype=jnp.int32)[None, :, None]
    select = jnp.any(hit, axis=0).astype(jnp.bfloat16)
    weight = jnp.sum(jnp.where(hit, gates_all.T[:, None, :], jnp.float32(0.0)), axis=0)

    buffer = jnp.dot(select, normed_all, preferred_element_type=jnp.float32).astype(jnp.bfloat16)
    full_gate = jnp.concatenate(gate_pieces, axis=2)
    full_up = jnp.concatenate(up_pieces, axis=2)
    received = lax.all_to_all(
        buffer.reshape(n_tp, cap2, width), "tp", split_axis=0, concat_axis=0, tiled=True
    )
    received, down_pieces = lax.optimization_barrier((received, down_pieces))
    full_down = jnp.concatenate(down_pieces, axis=2)
    served = expert_rows(received, full_gate, full_up, full_down)
    back = lax.all_to_all(served, "tp", split_axis=0, concat_axis=0, tiled=True).reshape(
        n_slots, width
    )

    weight_hi = weight.astype(jnp.bfloat16)
    weight_lo = (weight - weight_hi.astype(jnp.float32)).astype(jnp.bfloat16)
    contract = (((0,), (0,)), ((), ()))
    partial = lax.dot_general(
        weight_hi, back, contract, preferred_element_type=jnp.float32
    ) + lax.dot_general(weight_lo, back, contract, preferred_element_type=jnp.float32)
    mixture = lax.psum_scatter(
        partial.astype(jnp.bfloat16).reshape(n_ep, home_rows, width),
        "ep",
        scatter_dimension=0,
        tiled=True,
    )
    layer_out = (state + mixture.astype(jnp.float32).reshape(packs, share, width)).astype(
        jnp.bfloat16
    )
    return layer_out


def solution(mesh):
    body = functools.partial(
        shards, n_cp=mesh.shape["cp"], n_tp=mesh.shape["tp"], n_ep=mesh.shape["ep"]
    )
    return jax.shard_map(
        body,
        mesh=mesh,
        in_specs=(
            P("ep", "cp", "tp"),
            P("ep", "cp", "tp"),
            P("ep", "cp", "tp"),
            P("ep", "cp"),
            P(),
            P(),
            P("tp", "cp"),
            P("ep", "cp", None),
            P(),
            P(),
            P("ep", "cp", None),
            P(("tp", "ep"), None, "cp"),
            P(("tp", "ep"), None, "cp"),
            P(("tp", "ep"), None, "cp"),
        ),
        out_specs=P("ep", ("cp", "tp"), None),
        check_vma=False,
    )
```

```python
import functools

import jax
import jax.numpy as jnp
from jax import lax
from jax.sharding import PartitionSpec as P

HEAD_WIDTH = 128


def root_mean_scale(entries, gain):
    mean_sq = jnp.mean(entries * entries, axis=-1, keepdims=True)
    return entries * lax.rsqrt(mean_sq + 1e-06) * gain


def capacity(share, top_count, experts):
    return min(
        share, max(2, share * top_count // experts + max(1, share * top_count // (8 * experts)))
    )


def slot_numbers(ids, experts):
    flat_ids = ids.reshape(-1)
    table = (flat_ids[:, None] == jnp.arange(experts, dtype=jnp.int32)[None, :]).astype(jnp.int32)
    before = jnp.cumsum(table, axis=0) - table
    return jnp.sum(before * table, axis=1).reshape(ids.shape)


def route(state, ids, norm_gain, router_weight):
    normed = root_mean_scale(state, norm_gain).astype(jnp.bfloat16)
    logits = jnp.dot(normed, router_weight, preferred_element_type=jnp.float32)
    experts = router_weight.shape[1]
    picks = ids[:, :, None] == jnp.arange(experts, dtype=jnp.int32)[None, None, :]
    chosen = jnp.sum(jnp.where(picks, logits[:, None, :], jnp.float32(0.0)), axis=-1)
    raised = jnp.exp(chosen)
    return (normed, raised / jnp.sum(raised, axis=-1, keepdims=True))


def cp_pieces(x, n_cp):
    pieces = [x]
    for shift in range(1, n_cp):
        perm = [(i, (i + shift) % n_cp) for i in range(n_cp)]
        pieces.append(lax.ppermute(x, "cp", perm))
    return pieces


def expert_rows(received, full_gate, full_up, full_down):
    width = received.shape[-1]
    flat_rows = received.reshape(-1, width)
    gate_act = jnp.dot(flat_rows, full_gate[0], preferred_element_type=jnp.float32)
    up_act = jnp.dot(flat_rows, full_up[0], preferred_element_type=jnp.float32)
    hidden_act = (jax.nn.silu(gate_act) * up_act).astype(jnp.bfloat16)
    served = jnp.einsum(
        "rf,df->rd", hidden_act, full_down[0], preferred_element_type=jnp.float32
    ).astype(jnp.bfloat16)
    return served.reshape(received.shape)


def shards(
    query,
    keys,
    values,
    segment_ids,
    query_norm_gain,
    key_norm_gain,
    out_weight,
    residual,
    norm_gain,
    router_weight,
    expert_ids,
    expert_gate,
    expert_up,
    expert_down,
    *,
    n_cp,
    n_tp,
    n_ep,
):
    packs = query.shape[0]
    row_count = query.shape[1]
    head_count = query.shape[2] // HEAD_WIDTH
    width = residual.shape[2]
    experts = router_weight.shape[1]
    top_count = expert_ids.shape[2]
    score_scale = HEAD_WIDTH ** (-0.5)

    query_rows_normed = root_mean_scale(
        query.astype(jnp.float32).reshape(packs, row_count, head_count, HEAD_WIDTH), query_norm_gain
    ).astype(jnp.bfloat16)
    key_rows_normed = root_mean_scale(keys.astype(jnp.float32), key_norm_gain).astype(jnp.bfloat16)
    key_value = jnp.concatenate([key_rows_normed, values], axis=-1)
    kv_all = jnp.concatenate(cp_pieces(key_value, n_cp), axis=1)
    doc_all = jnp.concatenate(cp_pieces(segment_ids, n_cp), axis=1)
    key_piece = kv_all[..., :HEAD_WIDTH]
    value_piece = kv_all[..., HEAD_WIDTH:]
    scores = (
        jnp.einsum(
            "pshd,pnd->phsn", query_rows_normed, key_piece, preferred_element_type=jnp.float32
        )
        * score_scale
    )
    same_doc = segment_ids[:, :, None] == doc_all[:, None, :]
    probs = jnp.where(same_doc[:, None], jnp.exp(scores), jnp.float32(0.0))
    denom = jnp.sum(probs, axis=-1)
    probs_b = probs.astype(jnp.bfloat16)
    summed = jnp.einsum("phsn,pnd->pshd", probs_b, value_piece, preferred_element_type=jnp.float32)
    attn = (
        (summed / jnp.transpose(denom, (0, 2, 1))[:, :, :, None])
        .astype(jnp.bfloat16)
        .reshape(packs * row_count, head_count * HEAD_WIDTH)
    )
    share = row_count // n_tp
    tp_index = lax.axis_index("tp")
    ep_index = lax.axis_index("ep")
    cp_index = lax.axis_index("cp")
    cap = capacity(share, top_count, experts)
    weight_pieces = cp_pieces(out_weight, n_cp)
    summed_blocks = []
    for piece in weight_pieces:
        block = jnp.dot(attn, piece, preferred_element_type=jnp.float32).reshape(
            packs, row_count, piece.shape[1]
        )
        summed_blocks.append(
            lax.psum_scatter(block.astype(jnp.bfloat16), "tp", scatter_dimension=1, tiled=True)
        )
    blocks = jnp.stack(summed_blocks, axis=2).astype(jnp.float32)
    source_block = (cp_index - jnp.arange(n_cp, dtype=jnp.int32)) % n_cp
    picks_block = source_block[:, None] == jnp.arange(n_cp, dtype=jnp.int32)[None, :]
    projected = jnp.sum(
        jnp.where(picks_block[None, None, :, :, None], blocks[:, :, None, :, :], jnp.float32(0.0)),
        axis=3,
    ).reshape(packs, share, width)
    first_row = tp_index * share
    state = lax.dynamic_slice_in_dim(residual, first_row, share, 1).astype(jnp.float32) + projected
    local_ids = lax.dynamic_slice_in_dim(expert_ids, first_row, share, 1).reshape(
        packs * share, top_count
    )
    home_rows = packs * share
    normed = root_mean_scale(state.reshape(home_rows, width), norm_gain).astype(jnp.bfloat16)

    weight_pieces, expert_gate, expert_up, expert_down = lax.optimization_barrier(
        (weight_pieces, expert_gate, expert_up, expert_down)
    )
    gate_pieces = cp_pieces(expert_gate, n_cp)
    up_pieces = cp_pieces(expert_up, n_cp)
    down_pieces = cp_pieces(expert_down, n_cp)
    normed, gate_pieces = lax.optimization_barrier((normed, gate_pieces))

    lanes = 128
    id_lanes = jnp.pad(local_ids.astype(jnp.bfloat16), ((0, 0), (0, lanes - top_count)))
    rows_all = lax.all_gather(
        jnp.concatenate([normed, id_lanes], axis=1), "ep", axis=0, tiled=True
    )
    normed_all = rows_all[:, :width]
    ids_all = rows_all[:, width : width + top_count].astype(jnp.int32)
    logits = jnp.dot(normed_all, router_weight, preferred_element_type=jnp.float32)
    picks = ids_all[:, :, None] == jnp.arange(experts, dtype=jnp.int32)[None, None, :]
    raised = jnp.exp(jnp.sum(jnp.where(picks, logits[:, None, :], jnp.float32(0.0)), axis=-1))
    gates_all = raised / jnp.sum(raised, axis=-1, keepdims=True)

    gathered = n_ep * home_rows
    dev_cap = packs * cap
    cap2 = n_ep * dev_cap
    n_slots = n_tp * cap2
    mine = (ids_all % n_ep) == ep_index
    dest = ids_all // n_ep
    named = jnp.stack(
        [jnp.any(mine & (dest == j), axis=1) for j in range(n_tp)], axis=1
    ).astype(jnp.bfloat16)
    row_iota = jnp.arange(gathered, dtype=jnp.int32)
    earlier = (row_iota[:, None] > row_iota[None, :]).astype(jnp.bfloat16)
    rank = jnp.dot(earlier, named, preferred_element_type=jnp.float32).astype(jnp.int32)
    rank_of = jnp.sum(
        jnp.where(dest[:, :, None] == jnp.arange(n_tp, dtype=jnp.int32)[None, None, :],
                  rank[:, None, :], 0),
        axis=-1,
    )
    target = jnp.where(mine, dest * cap2 + rank_of, jnp.int32(-1)).T
    target, up_pieces = lax.optimization_barrier((target, up_pieces))
    hit = target[:, None, :] == jnp.arange(n_slots, dtype=jnp.int32)[None, :, None]
    select = jnp.any(hit, axis=0).astype(jnp.bfloat16)
    weight = jnp.sum(jnp.where(hit, gates_all.T[:, None, :], jnp.float32(0.0)), axis=0)

    buffer = jnp.dot(select, normed_all, preferred_element_type=jnp.float32).astype(jnp.bfloat16)
    full_gate = jnp.concatenate(gate_pieces, axis=2)
    full_up = jnp.concatenate(up_pieces, axis=2)
    received = lax.all_to_all(
        buffer.reshape(n_tp, cap2, width), "tp", split_axis=0, concat_axis=0, tiled=True
    )
    received, down_pieces = lax.optimization_barrier((received, down_pieces))
    full_down = jnp.concatenate(down_pieces, axis=2)
    served = expert_rows(received, full_gate, full_up, full_down)
    back = lax.all_to_all(served, "tp", split_axis=0, concat_axis=0, tiled=True).reshape(
        n_slots, width
    )

    weight_hi = weight.astype(jnp.bfloat16)
    weight_lo = (weight - weight_hi.astype(jnp.float32)).astype(jnp.bfloat16)
    contract = (((0,), (0,)), ((), ()))
    partial = lax.dot_general(
        weight_hi, back, contract, preferred_element_type=jnp.float32
    ) + lax.dot_general(weight_lo, back, contract, preferred_element_type=jnp.float32)
    mixture = lax.psum_scatter(
        partial.astype(jnp.bfloat16).reshape(n_ep, home_rows, width),
        "ep",
        scatter_dimension=0,
        tiled=True,
    )
    layer_out = (state + mixture.astype(jnp.float32).reshape(packs, share, width)).astype(
        jnp.bfloat16
    )
    return layer_out


def solution(mesh):
    body = functools.partial(
        shards, n_cp=mesh.shape["cp"], n_tp=mesh.shape["tp"], n_ep=mesh.shape["ep"]
    )
    return jax.shard_map(
        body,
        mesh=mesh,
        in_specs=(
            P("ep", "cp", "tp"),
            P("ep", "cp", "tp"),
            P("ep", "cp", "tp"),
            P("ep", "cp"),
            P(),
            P(),
            P("tp", "cp"),
            P("ep", "cp", None),
            P(),
            P(),
            P("ep", "cp", None),
            P(("tp", "ep"), None, "cp"),
            P(("tp", "ep"), None, "cp"),
            P(("tp", "ep"), None, "cp"),
        ),
        out_specs=P("ep", ("cp", "tp"), None),
        check_vma=False,
    )
```

```python
import functools

import jax
import jax.numpy as jnp
from jax import lax
from jax.sharding import PartitionSpec as P

HEAD_WIDTH = 128


def root_mean_scale(entries, gain):
    mean_sq = jnp.mean(entries * entries, axis=-1, keepdims=True)
    return entries * lax.rsqrt(mean_sq + 1e-06) * gain


def capacity(share, top_count, experts):
    return min(
        share, max(2, share * top_count // experts + max(1, share * top_count // (8 * experts)))
    )


def slot_numbers(ids, experts):
    flat_ids = ids.reshape(-1)
    table = (flat_ids[:, None] == jnp.arange(experts, dtype=jnp.int32)[None, :]).astype(jnp.int32)
    before = jnp.cumsum(table, axis=0) - table
    return jnp.sum(before * table, axis=1).reshape(ids.shape)


def route(state, ids, norm_gain, router_weight):
    normed = root_mean_scale(state, norm_gain).astype(jnp.bfloat16)
    logits = jnp.dot(normed, router_weight, preferred_element_type=jnp.float32)
    experts = router_weight.shape[1]
    picks = ids[:, :, None] == jnp.arange(experts, dtype=jnp.int32)[None, None, :]
    chosen = jnp.sum(jnp.where(picks, logits[:, None, :], jnp.float32(0.0)), axis=-1)
    raised = jnp.exp(chosen)
    return (normed, raised / jnp.sum(raised, axis=-1, keepdims=True))


def cp_pieces(x, n_cp):
    pieces = [x]
    for shift in range(1, n_cp):
        perm = [(i, (i + shift) % n_cp) for i in range(n_cp)]
        pieces.append(lax.ppermute(x, "cp", perm))
    return pieces


def expert_rows(received, full_gate, full_up, full_down):
    width = received.shape[-1]
    flat_rows = received.reshape(-1, width)
    gate_act = jnp.dot(flat_rows, full_gate[0], preferred_element_type=jnp.float32)
    up_act = jnp.dot(flat_rows, full_up[0], preferred_element_type=jnp.float32)
    hidden_act = (jax.nn.silu(gate_act) * up_act).astype(jnp.bfloat16)
    served = jnp.einsum(
        "rf,df->rd", hidden_act, full_down[0], preferred_element_type=jnp.float32
    ).astype(jnp.bfloat16)
    return served.reshape(received.shape)


def shards(
    query,
    keys,
    values,
    segment_ids,
    query_norm_gain,
    key_norm_gain,
    out_weight,
    residual,
    norm_gain,
    router_weight,
    expert_ids,
    expert_gate,
    expert_up,
    expert_down,
    *,
    n_cp,
    n_tp,
    n_ep,
):
    packs = query.shape[0]
    row_count = query.shape[1]
    head_count = query.shape[2] // HEAD_WIDTH
    width = residual.shape[2]
    experts = router_weight.shape[1]
    top_count = expert_ids.shape[2]
    score_scale = HEAD_WIDTH ** (-0.5)

    query_rows_normed = root_mean_scale(
        query.astype(jnp.float32).reshape(packs, row_count, head_count, HEAD_WIDTH), query_norm_gain
    ).astype(jnp.bfloat16)
    key_rows_normed = root_mean_scale(keys.astype(jnp.float32), key_norm_gain).astype(jnp.bfloat16)
    key_value = jnp.concatenate([key_rows_normed, values], axis=-1)
    kv_all = jnp.concatenate(cp_pieces(key_value, n_cp), axis=1)
    doc_all = jnp.concatenate(cp_pieces(segment_ids, n_cp), axis=1)
    key_piece = kv_all[..., :HEAD_WIDTH]
    value_piece = kv_all[..., HEAD_WIDTH:]
    scores = (
        jnp.einsum(
            "pshd,pnd->phsn", query_rows_normed, key_piece, preferred_element_type=jnp.float32
        )
        * score_scale
    )
    same_doc = segment_ids[:, :, None] == doc_all[:, None, :]
    probs = jnp.where(same_doc[:, None], jnp.exp(scores), jnp.float32(0.0))
    denom = jnp.sum(probs, axis=-1)
    probs_b = probs.astype(jnp.bfloat16)
    summed = jnp.einsum("phsn,pnd->pshd", probs_b, value_piece, preferred_element_type=jnp.float32)
    attn = (
        (summed / jnp.transpose(denom, (0, 2, 1))[:, :, :, None])
        .astype(jnp.bfloat16)
        .reshape(packs * row_count, head_count * HEAD_WIDTH)
    )
    share = row_count // n_tp
    tp_index = lax.axis_index("tp")
    ep_index = lax.axis_index("ep")
    cp_index = lax.axis_index("cp")
    cap = capacity(share, top_count, experts)
    weight_pieces = cp_pieces(out_weight, n_cp)
    summed_blocks = []
    for piece in weight_pieces:
        block = jnp.dot(attn, piece, preferred_element_type=jnp.float32).reshape(
            packs, row_count, piece.shape[1]
        )
        summed_blocks.append(
            lax.psum_scatter(block.astype(jnp.bfloat16), "tp", scatter_dimension=1, tiled=True)
        )
    blocks = jnp.stack(summed_blocks, axis=2).astype(jnp.float32)
    source_block = (cp_index - jnp.arange(n_cp, dtype=jnp.int32)) % n_cp
    picks_block = source_block[:, None] == jnp.arange(n_cp, dtype=jnp.int32)[None, :]
    projected = jnp.sum(
        jnp.where(picks_block[None, None, :, :, None], blocks[:, :, None, :, :], jnp.float32(0.0)),
        axis=3,
    ).reshape(packs, share, width)
    first_row = tp_index * share
    state = lax.dynamic_slice_in_dim(residual, first_row, share, 1).astype(jnp.float32) + projected
    local_ids = lax.dynamic_slice_in_dim(expert_ids, first_row, share, 1).reshape(
        packs * share, top_count
    )
    home_rows = packs * share
    normed = root_mean_scale(state.reshape(home_rows, width), norm_gain).astype(jnp.bfloat16)

    weight_pieces, expert_gate, expert_up, expert_down = lax.optimization_barrier(
        (weight_pieces, expert_gate, expert_up, expert_down)
    )
    gate_pieces = cp_pieces(expert_gate, n_cp)
    up_pieces = cp_pieces(expert_up, n_cp)
    down_pieces = cp_pieces(expert_down, n_cp)
    normed, gate_pieces = lax.optimization_barrier((normed, gate_pieces))

    lanes = 128
    cap2 = n_ep * cap
    n_slots = n_tp * cap2
    gathered = n_ep * share
    row_iota = jnp.arange(gathered, dtype=jnp.int32)
    earlier = (row_iota[:, None] > row_iota[None, :]).astype(jnp.bfloat16)
    contract = (((0,), (0,)), ((), ()))
    mixtures = []
    for chunk in range(packs):
        rows = normed[chunk * share : (chunk + 1) * share]
        ids = local_ids[chunk * share : (chunk + 1) * share]
        id_lanes = jnp.pad(ids.astype(jnp.bfloat16), ((0, 0), (0, lanes - top_count)))
        rows_all = lax.all_gather(
            jnp.concatenate([rows, id_lanes], axis=1), "ep", axis=0, tiled=True
        )
        normed_all = rows_all[:, :width]
        ids_all = rows_all[:, width : width + top_count].astype(jnp.int32)
        logits = jnp.dot(normed_all, router_weight, preferred_element_type=jnp.float32)
        picks = ids_all[:, :, None] == jnp.arange(experts, dtype=jnp.int32)[None, None, :]
        raised = jnp.exp(
            jnp.sum(jnp.where(picks, logits[:, None, :], jnp.float32(0.0)), axis=-1)
        )
        gates_all = raised / jnp.sum(raised, axis=-1, keepdims=True)
        mine = (ids_all % n_ep) == ep_index
        dest = ids_all // n_ep
        named = jnp.stack(
            [jnp.any(mine & (dest == j), axis=1) for j in range(n_tp)], axis=1
        ).astype(jnp.bfloat16)
        rank = jnp.dot(earlier, named, preferred_element_type=jnp.float32).astype(jnp.int32)
        rank_of = jnp.sum(
            jnp.where(dest[:, :, None] == jnp.arange(n_tp, dtype=jnp.int32)[None, None, :],
                      rank[:, None, :], 0),
            axis=-1,
        )
        target = jnp.where(mine, dest * cap2 + rank_of, jnp.int32(-1)).T
        if chunk == 0:
            target, up_pieces = lax.optimization_barrier((target, up_pieces))
            full_gate = jnp.concatenate(gate_pieces, axis=2)
            full_up = jnp.concatenate(up_pieces, axis=2)
        hit = target[:, None, :] == jnp.arange(n_slots, dtype=jnp.int32)[None, :, None]
        select = jnp.any(hit, axis=0).astype(jnp.bfloat16)
        weight = jnp.sum(jnp.where(hit, gates_all.T[:, None, :], jnp.float32(0.0)), axis=0)

        buffer = jnp.dot(select, normed_all, preferred_element_type=jnp.float32).astype(
            jnp.bfloat16
        )
        received = lax.all_to_all(
            buffer.reshape(n_tp, cap2, width), "tp", split_axis=0, concat_axis=0, tiled=True
        )
        if chunk == 0:
            received, down_pieces = lax.optimization_barrier((received, down_pieces))
            full_down = jnp.concatenate(down_pieces, axis=2)
        served = expert_rows(received, full_gate, full_up, full_down)
        back = lax.all_to_all(served, "tp", split_axis=0, concat_axis=0, tiled=True).reshape(
            n_slots, width
        )

        weight_hi = weight.astype(jnp.bfloat16)
        weight_lo = (weight - weight_hi.astype(jnp.float32)).astype(jnp.bfloat16)
        partial = lax.dot_general(
            weight_hi, back, contract, preferred_element_type=jnp.float32
        ) + lax.dot_general(weight_lo, back, contract, preferred_element_type=jnp.float32)
        mixtures.append(
            lax.psum_scatter(
                partial.astype(jnp.bfloat16).reshape(n_ep, share, width),
                "ep",
                scatter_dimension=0,
                tiled=True,
            )
        )
    mixture = jnp.concatenate(mixtures, axis=0).astype(jnp.float32)
    layer_out = (state + mixture).astype(jnp.bfloat16)
    return layer_out


def solution(mesh):
    body = functools.partial(
        shards, n_cp=mesh.shape["cp"], n_tp=mesh.shape["tp"], n_ep=mesh.shape["ep"]
    )
    return jax.shard_map(
        body,
        mesh=mesh,
        in_specs=(
            P("ep", "cp", "tp"),
            P("ep", "cp", "tp"),
            P("ep", "cp", "tp"),
            P("ep", "cp"),
            P(),
            P(),
            P("tp", "cp"),
            P("ep", "cp", None),
            P(),
            P(),
            P("ep", "cp", None),
            P(("tp", "ep"), None, "cp"),
            P(("tp", "ep"), None, "cp"),
            P(("tp", "ep"), None, "cp"),
        ),
        out_specs=P("ep", ("cp", "tp"), None),
        check_vma=False,
    )
```

```python
import functools

import jax
import jax.numpy as jnp
from jax import lax
from jax.sharding import PartitionSpec as P

HEAD_WIDTH = 128


def root_mean_scale(entries, gain):
    mean_sq = jnp.mean(entries * entries, axis=-1, keepdims=True)
    return entries * lax.rsqrt(mean_sq + 1e-06) * gain


def capacity(share, top_count, experts):
    return min(
        share, max(2, share * top_count // experts + max(1, share * top_count // (8 * experts)))
    )


def slot_numbers(ids, experts):
    flat_ids = ids.reshape(-1)
    table = (flat_ids[:, None] == jnp.arange(experts, dtype=jnp.int32)[None, :]).astype(jnp.int32)
    before = jnp.cumsum(table, axis=0) - table
    return jnp.sum(before * table, axis=1).reshape(ids.shape)


def route(state, ids, norm_gain, router_weight):
    normed = root_mean_scale(state, norm_gain).astype(jnp.bfloat16)
    logits = jnp.dot(normed, router_weight, preferred_element_type=jnp.float32)
    experts = router_weight.shape[1]
    picks = ids[:, :, None] == jnp.arange(experts, dtype=jnp.int32)[None, None, :]
    chosen = jnp.sum(jnp.where(picks, logits[:, None, :], jnp.float32(0.0)), axis=-1)
    raised = jnp.exp(chosen)
    return (normed, raised / jnp.sum(raised, axis=-1, keepdims=True))


def cp_pieces(x, n_cp):
    pieces = [x]
    for shift in range(1, n_cp):
        perm = [(i, (i + shift) % n_cp) for i in range(n_cp)]
        pieces.append(lax.ppermute(x, "cp", perm))
    return pieces


def expert_rows(received, full_gate, full_up, full_down):
    width = received.shape[-1]
    flat_rows = received.reshape(-1, width)
    gate_act = jnp.dot(flat_rows, full_gate[0], preferred_element_type=jnp.float32)
    up_act = jnp.dot(flat_rows, full_up[0], preferred_element_type=jnp.float32)
    hidden_act = (jax.nn.silu(gate_act) * up_act).astype(jnp.bfloat16)
    served = jnp.einsum(
        "rf,df->rd", hidden_act, full_down[0], preferred_element_type=jnp.float32
    ).astype(jnp.bfloat16)
    return served.reshape(received.shape)


def shards(
    query,
    keys,
    values,
    segment_ids,
    query_norm_gain,
    key_norm_gain,
    out_weight,
    residual,
    norm_gain,
    router_weight,
    expert_ids,
    expert_gate,
    expert_up,
    expert_down,
    *,
    n_cp,
    n_tp,
    n_ep,
):
    packs = query.shape[0]
    row_count = query.shape[1]
    head_count = query.shape[2] // HEAD_WIDTH
    width = residual.shape[2]
    experts = router_weight.shape[1]
    top_count = expert_ids.shape[2]
    score_scale = HEAD_WIDTH ** (-0.5)

    query_rows_normed = root_mean_scale(
        query.astype(jnp.float32).reshape(packs, row_count, head_count, HEAD_WIDTH), query_norm_gain
    ).astype(jnp.bfloat16)
    key_rows_normed = root_mean_scale(keys.astype(jnp.float32), key_norm_gain).astype(jnp.bfloat16)
    key_value = jnp.concatenate([key_rows_normed, values], axis=-1)
    kv_all = jnp.concatenate(cp_pieces(key_value, n_cp), axis=1)
    doc_all = jnp.concatenate(cp_pieces(segment_ids, n_cp), axis=1)
    key_piece = kv_all[..., :HEAD_WIDTH]
    value_piece = kv_all[..., HEAD_WIDTH:]
    scores = (
        jnp.einsum(
            "pshd,pnd->phsn", query_rows_normed, key_piece, preferred_element_type=jnp.float32
        )
        * score_scale
    )
    same_doc = segment_ids[:, :, None] == doc_all[:, None, :]
    probs = jnp.where(same_doc[:, None], jnp.exp(scores), jnp.float32(0.0))
    denom = jnp.sum(probs, axis=-1)
    probs_b = probs.astype(jnp.bfloat16)
    summed = jnp.einsum("phsn,pnd->pshd", probs_b, value_piece, preferred_element_type=jnp.float32)
    attn = (
        (summed / jnp.transpose(denom, (0, 2, 1))[:, :, :, None])
        .astype(jnp.bfloat16)
        .reshape(packs * row_count, head_count * HEAD_WIDTH)
    )
    share = row_count // n_tp
    tp_index = lax.axis_index("tp")
    ep_index = lax.axis_index("ep")
    cp_index = lax.axis_index("cp")
    cap = capacity(share, top_count, experts)
    weight_pieces = cp_pieces(out_weight, n_cp)
    summed_blocks = []
    for piece in weight_pieces:
        block = jnp.dot(attn, piece, preferred_element_type=jnp.float32).reshape(
            packs, row_count, piece.shape[1]
        )
        summed_blocks.append(
            lax.psum_scatter(block.astype(jnp.bfloat16), "tp", scatter_dimension=1, tiled=True)
        )
    blocks = jnp.stack(summed_blocks, axis=2).astype(jnp.float32)
    source_block = (cp_index - jnp.arange(n_cp, dtype=jnp.int32)) % n_cp
    picks_block = source_block[:, None] == jnp.arange(n_cp, dtype=jnp.int32)[None, :]
    projected = jnp.sum(
        jnp.where(picks_block[None, None, :, :, None], blocks[:, :, None, :, :], jnp.float32(0.0)),
        axis=3,
    ).reshape(packs, share, width)
    first_row = tp_index * share
    state = lax.dynamic_slice_in_dim(residual, first_row, share, 1).astype(jnp.float32) + projected
    local_ids = lax.dynamic_slice_in_dim(expert_ids, first_row, share, 1).reshape(
        packs * share, top_count
    )
    home_rows = packs * share
    normed = root_mean_scale(state.reshape(home_rows, width), norm_gain).astype(jnp.bfloat16)

    weight_pieces, expert_gate, expert_up, expert_down = lax.optimization_barrier(
        (weight_pieces, expert_gate, expert_up, expert_down)
    )
    gate_pieces = cp_pieces(expert_gate, n_cp)
    up_pieces = cp_pieces(expert_up, n_cp)
    down_pieces = cp_pieces(expert_down, n_cp)
    normed, gate_pieces = lax.optimization_barrier((normed, gate_pieces))

    lanes = 128
    cap2 = n_ep * cap
    n_slots = n_tp * cap2
    gathered = n_ep * share
    row_iota = jnp.arange(gathered, dtype=jnp.int32)
    earlier = (row_iota[:, None] > row_iota[None, :]).astype(jnp.bfloat16)
    contract = (((0,), (0,)), ((), ()))
    mixtures = []
    for chunk in range(packs):
        rows = normed[chunk * share : (chunk + 1) * share]
        ids = local_ids[chunk * share : (chunk + 1) * share]
        if chunk > 0:
            rows, ids, _ = lax.optimization_barrier((rows, ids, buffer))
        id_lanes = jnp.pad(ids.astype(jnp.bfloat16), ((0, 0), (0, lanes - top_count)))
        rows_all = lax.all_gather(
            jnp.concatenate([rows, id_lanes], axis=1), "ep", axis=0, tiled=True
        )
        normed_all = rows_all[:, :width]
        ids_all = rows_all[:, width : width + top_count].astype(jnp.int32)
        logits = jnp.dot(normed_all, router_weight, preferred_element_type=jnp.float32)
        picks = ids_all[:, :, None] == jnp.arange(experts, dtype=jnp.int32)[None, None, :]
        raised = jnp.exp(
            jnp.sum(jnp.where(picks, logits[:, None, :], jnp.float32(0.0)), axis=-1)
        )
        gates_all = raised / jnp.sum(raised, axis=-1, keepdims=True)
        mine = (ids_all % n_ep) == ep_index
        dest = ids_all // n_ep
        named = jnp.stack(
            [jnp.any(mine & (dest == j), axis=1) for j in range(n_tp)], axis=1
        ).astype(jnp.bfloat16)
        rank = jnp.dot(earlier, named, preferred_element_type=jnp.float32).astype(jnp.int32)
        rank_of = jnp.sum(
            jnp.where(dest[:, :, None] == jnp.arange(n_tp, dtype=jnp.int32)[None, None, :],
                      rank[:, None, :], 0),
            axis=-1,
        )
        target = jnp.where(mine, dest * cap2 + rank_of, jnp.int32(-1)).T
        if chunk == 0:
            target, up_pieces = lax.optimization_barrier((target, up_pieces))
            full_gate = jnp.concatenate(gate_pieces, axis=2)
            full_up = jnp.concatenate(up_pieces, axis=2)
        hit = target[:, None, :] == jnp.arange(n_slots, dtype=jnp.int32)[None, :, None]
        select = jnp.any(hit, axis=0).astype(jnp.bfloat16)
        weight = jnp.sum(jnp.where(hit, gates_all.T[:, None, :], jnp.float32(0.0)), axis=0)

        buffer = jnp.dot(select, normed_all, preferred_element_type=jnp.float32).astype(
            jnp.bfloat16
        )
        received = lax.all_to_all(
            buffer.reshape(n_tp, cap2, width), "tp", split_axis=0, concat_axis=0, tiled=True
        )
        if chunk == 0:
            received, down_pieces = lax.optimization_barrier((received, down_pieces))
            full_down = jnp.concatenate(down_pieces, axis=2)
        served = expert_rows(received, full_gate, full_up, full_down)
        back = lax.all_to_all(served, "tp", split_axis=0, concat_axis=0, tiled=True).reshape(
            n_slots, width
        )

        weight_hi = weight.astype(jnp.bfloat16)
        weight_lo = (weight - weight_hi.astype(jnp.float32)).astype(jnp.bfloat16)
        partial = lax.dot_general(
            weight_hi, back, contract, preferred_element_type=jnp.float32
        ) + lax.dot_general(weight_lo, back, contract, preferred_element_type=jnp.float32)
        mixtures.append(
            lax.psum_scatter(
                partial.astype(jnp.bfloat16).reshape(n_ep, share, width),
                "ep",
                scatter_dimension=0,
                tiled=True,
            )
        )
    mixture = jnp.concatenate(mixtures, axis=0).astype(jnp.float32)
    layer_out = (state + mixture).astype(jnp.bfloat16)
    return layer_out


def solution(mesh):
    body = functools.partial(
        shards, n_cp=mesh.shape["cp"], n_tp=mesh.shape["tp"], n_ep=mesh.shape["ep"]
    )
    return jax.shard_map(
        body,
        mesh=mesh,
        in_specs=(
            P("ep", "cp", "tp"),
            P("ep", "cp", "tp"),
            P("ep", "cp", "tp"),
            P("ep", "cp"),
            P(),
            P(),
            P("tp", "cp"),
            P("ep", "cp", None),
            P(),
            P(),
            P("ep", "cp", None),
            P(("tp", "ep"), None, "cp"),
            P(("tp", "ep"), None, "cp"),
            P(("tp", "ep"), None, "cp"),
        ),
        out_specs=P("ep", ("cp", "tp"), None),
        check_vma=False,
    )
```

```python
import functools

import jax
import jax.numpy as jnp
from jax import lax
from jax.sharding import PartitionSpec as P

HEAD_WIDTH = 128


def root_mean_scale(entries, gain):
    mean_sq = jnp.mean(entries * entries, axis=-1, keepdims=True)
    return entries * lax.rsqrt(mean_sq + 1e-06) * gain


def capacity(share, top_count, experts):
    return min(
        share, max(2, share * top_count // experts + max(1, share * top_count // (8 * experts)))
    )


def slot_numbers(ids, experts):
    flat_ids = ids.reshape(-1)
    table = (flat_ids[:, None] == jnp.arange(experts, dtype=jnp.int32)[None, :]).astype(jnp.int32)
    before = jnp.cumsum(table, axis=0) - table
    return jnp.sum(before * table, axis=1).reshape(ids.shape)


def route(state, ids, norm_gain, router_weight):
    normed = root_mean_scale(state, norm_gain).astype(jnp.bfloat16)
    logits = jnp.dot(normed, router_weight, preferred_element_type=jnp.float32)
    experts = router_weight.shape[1]
    picks = ids[:, :, None] == jnp.arange(experts, dtype=jnp.int32)[None, None, :]
    chosen = jnp.sum(jnp.where(picks, logits[:, None, :], jnp.float32(0.0)), axis=-1)
    raised = jnp.exp(chosen)
    return (normed, raised / jnp.sum(raised, axis=-1, keepdims=True))


def cp_pieces(x, n_cp):
    pieces = [x]
    for shift in range(1, n_cp):
        perm = [(i, (i + shift) % n_cp) for i in range(n_cp)]
        pieces.append(lax.ppermute(x, "cp", perm))
    return pieces


def sum_scatter(x, axis, size, dim):
    shape = x.shape
    parts = x.reshape(shape[:dim] + (size, shape[dim] // size) + shape[dim + 1 :])
    arrived = lax.all_to_all(parts, axis, split_axis=dim, concat_axis=dim, tiled=True)
    return jnp.sum(arrived.astype(jnp.float32), axis=dim)


def expert_rows(received, full_gate, full_up, full_down):
    width = received.shape[-1]
    flat_rows = received.reshape(-1, width)
    gate_act = jnp.dot(flat_rows, full_gate[0], preferred_element_type=jnp.float32)
    up_act = jnp.dot(flat_rows, full_up[0], preferred_element_type=jnp.float32)
    hidden_act = (jax.nn.silu(gate_act) * up_act).astype(jnp.bfloat16)
    served = jnp.einsum(
        "rf,df->rd", hidden_act, full_down[0], preferred_element_type=jnp.float32
    ).astype(jnp.bfloat16)
    return served.reshape(received.shape)


def shards(
    query,
    keys,
    values,
    segment_ids,
    query_norm_gain,
    key_norm_gain,
    out_weight,
    residual,
    norm_gain,
    router_weight,
    expert_ids,
    expert_gate,
    expert_up,
    expert_down,
    *,
    n_cp,
    n_tp,
    n_ep,
):
    packs = query.shape[0]
    row_count = query.shape[1]
    head_count = query.shape[2] // HEAD_WIDTH
    width = residual.shape[2]
    experts = router_weight.shape[1]
    top_count = expert_ids.shape[2]
    score_scale = HEAD_WIDTH ** (-0.5)

    query_rows_normed = root_mean_scale(
        query.astype(jnp.float32).reshape(packs, row_count, head_count, HEAD_WIDTH), query_norm_gain
    ).astype(jnp.bfloat16)
    key_rows_normed = root_mean_scale(keys.astype(jnp.float32), key_norm_gain).astype(jnp.bfloat16)
    key_value = jnp.concatenate([key_rows_normed, values], axis=-1)
    kv_all = jnp.concatenate(cp_pieces(key_value, n_cp), axis=1)
    doc_all = jnp.concatenate(cp_pieces(segment_ids, n_cp), axis=1)
    key_piece = kv_all[..., :HEAD_WIDTH]
    value_piece = kv_all[..., HEAD_WIDTH:]
    scores = (
        jnp.einsum(
            "pshd,pnd->phsn", query_rows_normed, key_piece, preferred_element_type=jnp.float32
        )
        * score_scale
    )
    same_doc = segment_ids[:, :, None] == doc_all[:, None, :]
    probs = jnp.where(same_doc[:, None], jnp.exp(scores), jnp.float32(0.0))
    denom = jnp.sum(probs, axis=-1)
    probs_b = probs.astype(jnp.bfloat16)
    summed = jnp.einsum("phsn,pnd->pshd", probs_b, value_piece, preferred_element_type=jnp.float32)
    attn = (
        (summed / jnp.transpose(denom, (0, 2, 1))[:, :, :, None])
        .astype(jnp.bfloat16)
        .reshape(packs * row_count, head_count * HEAD_WIDTH)
    )
    share = row_count // n_tp
    tp_index = lax.axis_index("tp")
    ep_index = lax.axis_index("ep")
    cp_index = lax.axis_index("cp")
    cap = capacity(share, top_count, experts)
    weight_pieces = cp_pieces(out_weight, n_cp)
    summed_blocks = []
    for j, piece in enumerate(weight_pieces):
        block = jnp.dot(attn, piece, preferred_element_type=jnp.float32).reshape(
            packs, row_count, piece.shape[1]
        )
        if j == 0:
            summed_blocks.append(
                lax.psum_scatter(block.astype(jnp.bfloat16), "tp", scatter_dimension=1, tiled=True)
            )
        else:
            summed_blocks.append(sum_scatter(block.astype(jnp.bfloat16), "tp", n_tp, 1))
    blocks = jnp.stack(summed_blocks, axis=2).astype(jnp.float32)
    source_block = (cp_index - jnp.arange(n_cp, dtype=jnp.int32)) % n_cp
    picks_block = source_block[:, None] == jnp.arange(n_cp, dtype=jnp.int32)[None, :]
    projected = jnp.sum(
        jnp.where(picks_block[None, None, :, :, None], blocks[:, :, None, :, :], jnp.float32(0.0)),
        axis=3,
    ).reshape(packs, share, width)
    first_row = tp_index * share
    state = lax.dynamic_slice_in_dim(residual, first_row, share, 1).astype(jnp.float32) + projected
    local_ids = lax.dynamic_slice_in_dim(expert_ids, first_row, share, 1).reshape(
        packs * share, top_count
    )
    home_rows = packs * share
    normed = root_mean_scale(state.reshape(home_rows, width), norm_gain).astype(jnp.bfloat16)

    weight_pieces, expert_gate, expert_up, expert_down = lax.optimization_barrier(
        (weight_pieces, expert_gate, expert_up, expert_down)
    )
    gate_pieces = cp_pieces(expert_gate, n_cp)
    up_pieces = cp_pieces(expert_up, n_cp)
    down_pieces = cp_pieces(expert_down, n_cp)
    normed, gate_pieces = lax.optimization_barrier((normed, gate_pieces))

    lanes = 128
    cap2 = n_ep * cap
    n_slots = n_tp * cap2
    gathered = n_ep * share
    row_iota = jnp.arange(gathered, dtype=jnp.int32)
    earlier = (row_iota[:, None] > row_iota[None, :]).astype(jnp.bfloat16)
    contract = (((0,), (0,)), ((), ()))
    mixtures = []
    for chunk in range(packs):
        rows = normed[chunk * share : (chunk + 1) * share]
        ids = local_ids[chunk * share : (chunk + 1) * share]
        if chunk > 0:
            rows, ids, _ = lax.optimization_barrier((rows, ids, buffer))
        id_lanes = jnp.pad(ids.astype(jnp.bfloat16), ((0, 0), (0, lanes - top_count)))
        rows_all = lax.all_gather(
            jnp.concatenate([rows, id_lanes], axis=1), "ep", axis=0, tiled=True
        )
        normed_all = rows_all[:, :width]
        ids_all = rows_all[:, width : width + top_count].astype(jnp.int32)
        logits = jnp.dot(normed_all, router_weight, preferred_element_type=jnp.float32)
        picks = ids_all[:, :, None] == jnp.arange(experts, dtype=jnp.int32)[None, None, :]
        raised = jnp.exp(
            jnp.sum(jnp.where(picks, logits[:, None, :], jnp.float32(0.0)), axis=-1)
        )
        gates_all = raised / jnp.sum(raised, axis=-1, keepdims=True)
        mine = (ids_all % n_ep) == ep_index
        dest = ids_all // n_ep
        named = jnp.stack(
            [jnp.any(mine & (dest == j), axis=1) for j in range(n_tp)], axis=1
        ).astype(jnp.bfloat16)
        rank = jnp.dot(earlier, named, preferred_element_type=jnp.float32).astype(jnp.int32)
        rank_of = jnp.sum(
            jnp.where(dest[:, :, None] == jnp.arange(n_tp, dtype=jnp.int32)[None, None, :],
                      rank[:, None, :], 0),
            axis=-1,
        )
        target = jnp.where(mine, dest * cap2 + rank_of, jnp.int32(-1)).T
        if chunk == 0:
            target, up_pieces = lax.optimization_barrier((target, up_pieces))
            full_gate = jnp.concatenate(gate_pieces, axis=2)
            full_up = jnp.concatenate(up_pieces, axis=2)
        hit = target[:, None, :] == jnp.arange(n_slots, dtype=jnp.int32)[None, :, None]
        select = jnp.any(hit, axis=0).astype(jnp.bfloat16)
        weight = jnp.sum(jnp.where(hit, gates_all.T[:, None, :], jnp.float32(0.0)), axis=0)

        buffer = jnp.dot(select, normed_all, preferred_element_type=jnp.float32).astype(
            jnp.bfloat16
        )
        received = lax.all_to_all(
            buffer.reshape(n_tp, cap2, width), "tp", split_axis=0, concat_axis=0, tiled=True
        )
        if chunk == 0:
            received, down_pieces = lax.optimization_barrier((received, down_pieces))
            full_down = jnp.concatenate(down_pieces, axis=2)
        served = expert_rows(received, full_gate, full_up, full_down)
        back = lax.all_to_all(served, "tp", split_axis=0, concat_axis=0, tiled=True).reshape(
            n_slots, width
        )

        weight_hi = weight.astype(jnp.bfloat16)
        weight_lo = (weight - weight_hi.astype(jnp.float32)).astype(jnp.bfloat16)
        partial = lax.dot_general(
            weight_hi, back, contract, preferred_element_type=jnp.float32
        ) + lax.dot_general(weight_lo, back, contract, preferred_element_type=jnp.float32)
        partial = partial.astype(jnp.bfloat16).reshape(n_ep, share, width)
        if chunk < packs - 1:
            mixtures.append(
                lax.psum_scatter(partial, "ep", scatter_dimension=0, tiled=True).astype(
                    jnp.float32
                )
            )
        else:
            mixtures.append(sum_scatter(partial, "ep", n_ep, 0))
    mixture = jnp.concatenate(mixtures, axis=0).astype(jnp.float32)
    layer_out = (state + mixture).astype(jnp.bfloat16)
    return layer_out


def solution(mesh):
    body = functools.partial(
        shards, n_cp=mesh.shape["cp"], n_tp=mesh.shape["tp"], n_ep=mesh.shape["ep"]
    )
    return jax.shard_map(
        body,
        mesh=mesh,
        in_specs=(
            P("ep", "cp", "tp"),
            P("ep", "cp", "tp"),
            P("ep", "cp", "tp"),
            P("ep", "cp"),
            P(),
            P(),
            P("tp", "cp"),
            P("ep", "cp", None),
            P(),
            P(),
            P("ep", "cp", None),
            P(("tp", "ep"), None, "cp"),
            P(("tp", "ep"), None, "cp"),
            P(("tp", "ep"), None, "cp"),
        ),
        out_specs=P("ep", ("cp", "tp"), None),
        check_vma=False,
    )
```

```python
import functools

import jax
import jax.numpy as jnp
from jax import lax
from jax.sharding import PartitionSpec as P

HEAD_WIDTH = 128


def root_mean_scale(entries, gain):
    mean_sq = jnp.mean(entries * entries, axis=-1, keepdims=True)
    return entries * lax.rsqrt(mean_sq + 1e-06) * gain


def capacity(share, top_count, experts):
    return min(
        share, max(2, share * top_count // experts + max(1, share * top_count // (8 * experts)))
    )


def slot_numbers(ids, experts):
    flat_ids = ids.reshape(-1)
    table = (flat_ids[:, None] == jnp.arange(experts, dtype=jnp.int32)[None, :]).astype(jnp.int32)
    before = jnp.cumsum(table, axis=0) - table
    return jnp.sum(before * table, axis=1).reshape(ids.shape)


def route(state, ids, norm_gain, router_weight):
    normed = root_mean_scale(state, norm_gain).astype(jnp.bfloat16)
    logits = jnp.dot(normed, router_weight, preferred_element_type=jnp.float32)
    experts = router_weight.shape[1]
    picks = ids[:, :, None] == jnp.arange(experts, dtype=jnp.int32)[None, None, :]
    chosen = jnp.sum(jnp.where(picks, logits[:, None, :], jnp.float32(0.0)), axis=-1)
    raised = jnp.exp(chosen)
    return (normed, raised / jnp.sum(raised, axis=-1, keepdims=True))


def cp_pieces(x, n_cp):
    pieces = [x]
    for shift in range(1, n_cp):
        perm = [(i, (i + shift) % n_cp) for i in range(n_cp)]
        pieces.append(lax.ppermute(x, "cp", perm))
    return pieces


def expert_rows(received, full_gate, full_up, full_down):
    width = received.shape[-1]
    flat_rows = received.reshape(-1, width)
    gate_act = jnp.dot(flat_rows, full_gate[0], preferred_element_type=jnp.float32)
    up_act = jnp.dot(flat_rows, full_up[0], preferred_element_type=jnp.float32)
    hidden_act = (jax.nn.silu(gate_act) * up_act).astype(jnp.bfloat16)
    served = jnp.einsum(
        "rf,df->rd", hidden_act, full_down[0], preferred_element_type=jnp.float32
    ).astype(jnp.bfloat16)
    return served.reshape(received.shape)


def shards(
    query,
    keys,
    values,
    segment_ids,
    query_norm_gain,
    key_norm_gain,
    out_weight,
    residual,
    norm_gain,
    router_weight,
    expert_ids,
    expert_gate,
    expert_up,
    expert_down,
    *,
    n_cp,
    n_tp,
    n_ep,
):
    packs = query.shape[0]
    row_count = query.shape[1]
    head_count = query.shape[2] // HEAD_WIDTH
    width = residual.shape[2]
    experts = router_weight.shape[1]
    top_count = expert_ids.shape[2]
    score_scale = HEAD_WIDTH ** (-0.5)

    query_rows_normed = root_mean_scale(
        query.astype(jnp.float32).reshape(packs, row_count, head_count, HEAD_WIDTH), query_norm_gain
    ).astype(jnp.bfloat16)
    key_rows_normed = root_mean_scale(keys.astype(jnp.float32), key_norm_gain).astype(jnp.bfloat16)
    key_value = jnp.concatenate([key_rows_normed, values], axis=-1)
    kv_all = jnp.concatenate(cp_pieces(key_value, n_cp), axis=1)
    doc_all = jnp.concatenate(cp_pieces(segment_ids, n_cp), axis=1)
    key_piece = kv_all[..., :HEAD_WIDTH]
    value_piece = kv_all[..., HEAD_WIDTH:]
    scores = (
        jnp.einsum(
            "pshd,pnd->phsn", query_rows_normed, key_piece, preferred_element_type=jnp.float32
        )
        * score_scale
    )
    same_doc = segment_ids[:, :, None] == doc_all[:, None, :]
    probs = jnp.where(same_doc[:, None], jnp.exp(scores), jnp.float32(0.0))
    denom = jnp.sum(probs, axis=-1)
    probs_b = probs.astype(jnp.bfloat16)
    summed = jnp.einsum("phsn,pnd->pshd", probs_b, value_piece, preferred_element_type=jnp.float32)
    attn = (
        (summed / jnp.transpose(denom, (0, 2, 1))[:, :, :, None])
        .astype(jnp.bfloat16)
        .reshape(packs * row_count, head_count * HEAD_WIDTH)
    )
    share = row_count // n_tp
    tp_index = lax.axis_index("tp")
    ep_index = lax.axis_index("ep")
    cp_index = lax.axis_index("cp")
    cap = capacity(share, top_count, experts)
    attn_pieces = cp_pieces(attn, n_cp)
    received_blocks = []
    for j, piece in enumerate(attn_pieces):
        if j > 0:
            piece, received_blocks[0] = lax.optimization_barrier((piece, received_blocks[0]))
        block = jnp.dot(piece, out_weight, preferred_element_type=jnp.float32).reshape(
            packs, row_count, out_weight.shape[1]
        )
        summed = lax.psum_scatter(
            block.astype(jnp.bfloat16), "tp", scatter_dimension=1, tiled=True
        )
        if j > 0:
            summed = lax.ppermute(summed, "cp", [(i, (i - j) % n_cp) for i in range(n_cp)])
        received_blocks.append(summed)
    blocks = jnp.stack(received_blocks, axis=2).astype(jnp.float32)
    source_block = (jnp.arange(n_cp, dtype=jnp.int32) - cp_index) % n_cp
    picks_block = source_block[:, None] == jnp.arange(n_cp, dtype=jnp.int32)[None, :]
    projected = jnp.sum(
        jnp.where(picks_block[None, None, :, :, None], blocks[:, :, None, :, :], jnp.float32(0.0)),
        axis=3,
    ).reshape(packs, share, width)
    first_row = tp_index * share
    state = lax.dynamic_slice_in_dim(residual, first_row, share, 1).astype(jnp.float32) + projected
    local_ids = lax.dynamic_slice_in_dim(expert_ids, first_row, share, 1).reshape(
        packs * share, top_count
    )
    home_rows = packs * share
    normed = root_mean_scale(state.reshape(home_rows, width), norm_gain).astype(jnp.bfloat16)

    attn_pieces, expert_gate, expert_up, expert_down = lax.optimization_barrier(
        (attn_pieces, expert_gate, expert_up, expert_down)
    )
    gate_pieces = cp_pieces(expert_gate, n_cp)
    up_pieces = cp_pieces(expert_up, n_cp)
    down_pieces = cp_pieces(expert_down, n_cp)
    normed, gate_pieces = lax.optimization_barrier((normed, gate_pieces))

    lanes = 128
    cap2 = n_ep * cap
    n_slots = n_tp * cap2
    gathered = n_ep * share
    row_iota = jnp.arange(gathered, dtype=jnp.int32)
    earlier = (row_iota[:, None] > row_iota[None, :]).astype(jnp.bfloat16)
    contract = (((0,), (0,)), ((), ()))
    mixtures = []
    for chunk in range(packs):
        rows = normed[chunk * share : (chunk + 1) * share]
        ids = local_ids[chunk * share : (chunk + 1) * share]
        if chunk > 0:
            rows, ids, _ = lax.optimization_barrier((rows, ids, buffer))
        id_lanes = jnp.pad(ids.astype(jnp.bfloat16), ((0, 0), (0, lanes - top_count)))
        rows_all = lax.all_gather(
            jnp.concatenate([rows, id_lanes], axis=1), "ep", axis=0, tiled=True
        )
        normed_all = rows_all[:, :width]
        ids_all = rows_all[:, width : width + top_count].astype(jnp.int32)
        logits = jnp.dot(normed_all, router_weight, preferred_element_type=jnp.float32)
        picks = ids_all[:, :, None] == jnp.arange(experts, dtype=jnp.int32)[None, None, :]
        raised = jnp.exp(
            jnp.sum(jnp.where(picks, logits[:, None, :], jnp.float32(0.0)), axis=-1)
        )
        gates_all = raised / jnp.sum(raised, axis=-1, keepdims=True)
        mine = (ids_all % n_ep) == ep_index
        dest = ids_all // n_ep
        named = jnp.stack(
            [jnp.any(mine & (dest == j), axis=1) for j in range(n_tp)], axis=1
        ).astype(jnp.bfloat16)
        rank = jnp.dot(earlier, named, preferred_element_type=jnp.float32).astype(jnp.int32)
        rank_of = jnp.sum(
            jnp.where(dest[:, :, None] == jnp.arange(n_tp, dtype=jnp.int32)[None, None, :],
                      rank[:, None, :], 0),
            axis=-1,
        )
        target = jnp.where(mine, dest * cap2 + rank_of, jnp.int32(-1)).T
        if chunk == 0:
            target, up_pieces = lax.optimization_barrier((target, up_pieces))
            full_gate = jnp.concatenate(gate_pieces, axis=2)
            full_up = jnp.concatenate(up_pieces, axis=2)
        hit = target[:, None, :] == jnp.arange(n_slots, dtype=jnp.int32)[None, :, None]
        select = jnp.any(hit, axis=0).astype(jnp.bfloat16)
        weight = jnp.sum(jnp.where(hit, gates_all.T[:, None, :], jnp.float32(0.0)), axis=0)

        buffer = jnp.dot(select, normed_all, preferred_element_type=jnp.float32).astype(
            jnp.bfloat16
        )
        received = lax.all_to_all(
            buffer.reshape(n_tp, cap2, width), "tp", split_axis=0, concat_axis=0, tiled=True
        )
        if chunk == 0:
            received, down_pieces = lax.optimization_barrier((received, down_pieces))
            full_down = jnp.concatenate(down_pieces, axis=2)
        served = expert_rows(received, full_gate, full_up, full_down)
        back = lax.all_to_all(served, "tp", split_axis=0, concat_axis=0, tiled=True).reshape(
            n_slots, width
        )

        weight_hi = weight.astype(jnp.bfloat16)
        weight_lo = (weight - weight_hi.astype(jnp.float32)).astype(jnp.bfloat16)
        partial = lax.dot_general(
            weight_hi, back, contract, preferred_element_type=jnp.float32
        ) + lax.dot_general(weight_lo, back, contract, preferred_element_type=jnp.float32)
        mixtures.append(
            lax.psum_scatter(
                partial.astype(jnp.bfloat16).reshape(n_ep, share, width),
                "ep",
                scatter_dimension=0,
                tiled=True,
            )
        )
    mixture = jnp.concatenate(mixtures, axis=0).astype(jnp.float32)
    layer_out = (state + mixture).astype(jnp.bfloat16)
    return layer_out


def solution(mesh):
    body = functools.partial(
        shards, n_cp=mesh.shape["cp"], n_tp=mesh.shape["tp"], n_ep=mesh.shape["ep"]
    )
    return jax.shard_map(
        body,
        mesh=mesh,
        in_specs=(
            P("ep", "cp", "tp"),
            P("ep", "cp", "tp"),
            P("ep", "cp", "tp"),
            P("ep", "cp"),
            P(),
            P(),
            P("tp", "cp"),
            P("ep", "cp", None),
            P(),
            P(),
            P("ep", "cp", None),
            P(("tp", "ep"), None, "cp"),
            P(("tp", "ep"), None, "cp"),
            P(("tp", "ep"), None, "cp"),
        ),
        out_specs=P("ep", ("cp", "tp"), None),
        check_vma=False,
    )
```

```python
import functools

import jax
import jax.numpy as jnp
from jax import lax
from jax.sharding import PartitionSpec as P

HEAD_WIDTH = 128


def root_mean_scale(entries, gain):
    mean_sq = jnp.mean(entries * entries, axis=-1, keepdims=True)
    return entries * lax.rsqrt(mean_sq + 1e-06) * gain


def capacity(share, top_count, experts):
    return min(
        share, max(2, share * top_count // experts + max(1, share * top_count // (8 * experts)))
    )


def slot_numbers(ids, experts):
    flat_ids = ids.reshape(-1)
    table = (flat_ids[:, None] == jnp.arange(experts, dtype=jnp.int32)[None, :]).astype(jnp.int32)
    before = jnp.cumsum(table, axis=0) - table
    return jnp.sum(before * table, axis=1).reshape(ids.shape)


def route(state, ids, norm_gain, router_weight):
    normed = root_mean_scale(state, norm_gain).astype(jnp.bfloat16)
    logits = jnp.dot(normed, router_weight, preferred_element_type=jnp.float32)
    experts = router_weight.shape[1]
    picks = ids[:, :, None] == jnp.arange(experts, dtype=jnp.int32)[None, None, :]
    chosen = jnp.sum(jnp.where(picks, logits[:, None, :], jnp.float32(0.0)), axis=-1)
    raised = jnp.exp(chosen)
    return (normed, raised / jnp.sum(raised, axis=-1, keepdims=True))


def cp_pieces(x, n_cp):
    pieces = [x]
    for shift in range(1, n_cp):
        perm = [(i, (i + shift) % n_cp) for i in range(n_cp)]
        pieces.append(lax.ppermute(x, "cp", perm))
    return pieces


def expert_rows(received, full_gate, full_up, full_down):
    width = received.shape[-1]
    flat_rows = received.reshape(-1, width)
    gate_act = jnp.dot(flat_rows, full_gate[0], preferred_element_type=jnp.float32)
    up_act = jnp.dot(flat_rows, full_up[0], preferred_element_type=jnp.float32)
    hidden_act = (jax.nn.silu(gate_act) * up_act).astype(jnp.bfloat16)
    served = jnp.einsum(
        "rf,df->rd", hidden_act, full_down[0], preferred_element_type=jnp.float32
    ).astype(jnp.bfloat16)
    return served.reshape(received.shape)


def shards(
    query,
    keys,
    values,
    segment_ids,
    query_norm_gain,
    key_norm_gain,
    out_weight,
    residual,
    norm_gain,
    router_weight,
    expert_ids,
    expert_gate,
    expert_up,
    expert_down,
    *,
    n_cp,
    n_tp,
    n_ep,
):
    packs = query.shape[0]
    row_count = query.shape[1]
    head_count = query.shape[2] // HEAD_WIDTH
    width = residual.shape[2]
    experts = router_weight.shape[1]
    top_count = expert_ids.shape[2]
    score_scale = HEAD_WIDTH ** (-0.5)

    query_rows_normed = root_mean_scale(
        query.astype(jnp.float32).reshape(packs, row_count, head_count, HEAD_WIDTH), query_norm_gain
    ).astype(jnp.bfloat16)
    key_rows_normed = root_mean_scale(keys.astype(jnp.float32), key_norm_gain).astype(jnp.bfloat16)
    key_value = jnp.concatenate([key_rows_normed, values], axis=-1)
    kv_all = jnp.concatenate(cp_pieces(key_value, n_cp), axis=1)
    doc_all = jnp.concatenate(cp_pieces(segment_ids, n_cp), axis=1)
    key_piece = kv_all[..., :HEAD_WIDTH]
    value_piece = kv_all[..., HEAD_WIDTH:]
    scores = (
        jnp.einsum(
            "pshd,pnd->phsn", query_rows_normed, key_piece, preferred_element_type=jnp.float32
        )
        * score_scale
    )
    same_doc = segment_ids[:, :, None] == doc_all[:, None, :]
    probs = jnp.where(same_doc[:, None], jnp.exp(scores), jnp.float32(0.0))
    denom = jnp.sum(probs, axis=-1)
    probs_b = probs.astype(jnp.bfloat16)
    summed = jnp.einsum("phsn,pnd->pshd", probs_b, value_piece, preferred_element_type=jnp.float32)
    attn = (
        (summed / jnp.transpose(denom, (0, 2, 1))[:, :, :, None])
        .astype(jnp.bfloat16)
        .reshape(packs * row_count, head_count * HEAD_WIDTH)
    )
    share = row_count // n_tp
    tp_index = lax.axis_index("tp")
    ep_index = lax.axis_index("ep")
    cp_index = lax.axis_index("cp")
    cap = capacity(share, top_count, experts)
    gate_head = expert_gate[:, :, : expert_gate.shape[2] // 2]
    gate_tail = expert_gate[:, :, expert_gate.shape[2] // 2 :]
    gate_head_pieces = cp_pieces(gate_head, n_cp)
    attn, gate_head_pieces = lax.optimization_barrier((attn, gate_head_pieces))
    attn_pieces = cp_pieces(attn, n_cp)
    received_blocks = []
    for j, piece in enumerate(attn_pieces):
        if j > 0:
            piece, received_blocks[0] = lax.optimization_barrier((piece, received_blocks[0]))
        block = jnp.dot(piece, out_weight, preferred_element_type=jnp.float32).reshape(
            packs, row_count, out_weight.shape[1]
        )
        summed = lax.psum_scatter(
            block.astype(jnp.bfloat16), "tp", scatter_dimension=1, tiled=True
        )
        if j > 0:
            summed = lax.ppermute(summed, "cp", [(i, (i - j) % n_cp) for i in range(n_cp)])
        received_blocks.append(summed)
    blocks = jnp.stack(received_blocks, axis=2).astype(jnp.float32)
    source_block = (jnp.arange(n_cp, dtype=jnp.int32) - cp_index) % n_cp
    picks_block = source_block[:, None] == jnp.arange(n_cp, dtype=jnp.int32)[None, :]
    projected = jnp.sum(
        jnp.where(picks_block[None, None, :, :, None], blocks[:, :, None, :, :], jnp.float32(0.0)),
        axis=3,
    ).reshape(packs, share, width)
    first_row = tp_index * share
    state = lax.dynamic_slice_in_dim(residual, first_row, share, 1).astype(jnp.float32) + projected
    local_ids = lax.dynamic_slice_in_dim(expert_ids, first_row, share, 1).reshape(
        packs * share, top_count
    )
    home_rows = packs * share
    normed = root_mean_scale(state.reshape(home_rows, width), norm_gain).astype(jnp.bfloat16)

    attn_pieces, gate_tail, expert_up, expert_down = lax.optimization_barrier(
        (attn_pieces, gate_tail, expert_up, expert_down)
    )
    gate_tail_pieces = cp_pieces(gate_tail, n_cp)
    gate_pieces = [
        jnp.concatenate([head, tail], axis=2)
        for head, tail in zip(gate_head_pieces, gate_tail_pieces)
    ]
    up_pieces = cp_pieces(expert_up, n_cp)
    down_pieces = cp_pieces(expert_down, n_cp)
    normed, gate_pieces = lax.optimization_barrier((normed, gate_pieces))

    lanes = 128
    cap2 = n_ep * cap
    n_slots = n_tp * cap2
    gathered = n_ep * share
    row_iota = jnp.arange(gathered, dtype=jnp.int32)
    earlier = (row_iota[:, None] > row_iota[None, :]).astype(jnp.bfloat16)
    contract = (((0,), (0,)), ((), ()))
    mixtures = []
    for chunk in range(packs):
        rows = normed[chunk * share : (chunk + 1) * share]
        ids = local_ids[chunk * share : (chunk + 1) * share]
        if chunk > 0:
            rows, ids, _ = lax.optimization_barrier((rows, ids, buffer))
        id_lanes = jnp.pad(ids.astype(jnp.bfloat16), ((0, 0), (0, lanes - top_count)))
        rows_all = lax.all_gather(
            jnp.concatenate([rows, id_lanes], axis=1), "ep", axis=0, tiled=True
        )
        normed_all = rows_all[:, :width]
        ids_all = rows_all[:, width : width + top_count].astype(jnp.int32)
        logits = jnp.dot(normed_all, router_weight, preferred_element_type=jnp.float32)
        picks = ids_all[:, :, None] == jnp.arange(experts, dtype=jnp.int32)[None, None, :]
        raised = jnp.exp(
            jnp.sum(jnp.where(picks, logits[:, None, :], jnp.float32(0.0)), axis=-1)
        )
        gates_all = raised / jnp.sum(raised, axis=-1, keepdims=True)
        mine = (ids_all % n_ep) == ep_index
        dest = ids_all // n_ep
        named = jnp.stack(
            [jnp.any(mine & (dest == j), axis=1) for j in range(n_tp)], axis=1
        ).astype(jnp.bfloat16)
        rank = jnp.dot(earlier, named, preferred_element_type=jnp.float32).astype(jnp.int32)
        rank_of = jnp.sum(
            jnp.where(dest[:, :, None] == jnp.arange(n_tp, dtype=jnp.int32)[None, None, :],
                      rank[:, None, :], 0),
            axis=-1,
        )
        target = jnp.where(mine, dest * cap2 + rank_of, jnp.int32(-1)).T
        if chunk == 0:
            target, up_pieces = lax.optimization_barrier((target, up_pieces))
            full_gate = jnp.concatenate(gate_pieces, axis=2)
            full_up = jnp.concatenate(up_pieces, axis=2)
        hit = target[:, None, :] == jnp.arange(n_slots, dtype=jnp.int32)[None, :, None]
        select = jnp.any(hit, axis=0).astype(jnp.bfloat16)
        weight = jnp.sum(jnp.where(hit, gates_all.T[:, None, :], jnp.float32(0.0)), axis=0)

        buffer = jnp.dot(select, normed_all, preferred_element_type=jnp.float32).astype(
            jnp.bfloat16
        )
        received = lax.all_to_all(
            buffer.reshape(n_tp, cap2, width), "tp", split_axis=0, concat_axis=0, tiled=True
        )
        if chunk == 0:
            received, down_pieces = lax.optimization_barrier((received, down_pieces))
            full_down = jnp.concatenate(down_pieces, axis=2)
        served = expert_rows(received, full_gate, full_up, full_down)
        back = lax.all_to_all(served, "tp", split_axis=0, concat_axis=0, tiled=True).reshape(
            n_slots, width
        )

        weight_hi = weight.astype(jnp.bfloat16)
        weight_lo = (weight - weight_hi.astype(jnp.float32)).astype(jnp.bfloat16)
        partial = lax.dot_general(
            weight_hi, back, contract, preferred_element_type=jnp.float32
        ) + lax.dot_general(weight_lo, back, contract, preferred_element_type=jnp.float32)
        mixtures.append(
            lax.psum_scatter(
                partial.astype(jnp.bfloat16).reshape(n_ep, share, width),
                "ep",
                scatter_dimension=0,
                tiled=True,
            )
        )
    mixture = jnp.concatenate(mixtures, axis=0).astype(jnp.float32)
    layer_out = (state + mixture).astype(jnp.bfloat16)
    return layer_out


def solution(mesh):
    body = functools.partial(
        shards, n_cp=mesh.shape["cp"], n_tp=mesh.shape["tp"], n_ep=mesh.shape["ep"]
    )
    return jax.shard_map(
        body,
        mesh=mesh,
        in_specs=(
            P("ep", "cp", "tp"),
            P("ep", "cp", "tp"),
            P("ep", "cp", "tp"),
            P("ep", "cp"),
            P(),
            P(),
            P("tp", "cp"),
            P("ep", "cp", None),
            P(),
            P(),
            P("ep", "cp", None),
            P(("tp", "ep"), None, "cp"),
            P(("tp", "ep"), None, "cp"),
            P(("tp", "ep"), None, "cp"),
        ),
        out_specs=P("ep", ("cp", "tp"), None),
        check_vma=False,
    )
```

```python
import functools

import jax
import jax.numpy as jnp
from jax import lax
from jax.sharding import PartitionSpec as P

HEAD_WIDTH = 128


def root_mean_scale(entries, gain):
    mean_sq = jnp.mean(entries * entries, axis=-1, keepdims=True)
    return entries * lax.rsqrt(mean_sq + 1e-06) * gain


def capacity(share, top_count, experts):
    return min(
        share, max(2, share * top_count // experts + max(1, share * top_count // (8 * experts)))
    )


def slot_numbers(ids, experts):
    flat_ids = ids.reshape(-1)
    table = (flat_ids[:, None] == jnp.arange(experts, dtype=jnp.int32)[None, :]).astype(jnp.int32)
    before = jnp.cumsum(table, axis=0) - table
    return jnp.sum(before * table, axis=1).reshape(ids.shape)


def route(state, ids, norm_gain, router_weight):
    normed = root_mean_scale(state, norm_gain).astype(jnp.bfloat16)
    logits = jnp.dot(normed, router_weight, preferred_element_type=jnp.float32)
    experts = router_weight.shape[1]
    picks = ids[:, :, None] == jnp.arange(experts, dtype=jnp.int32)[None, None, :]
    chosen = jnp.sum(jnp.where(picks, logits[:, None, :], jnp.float32(0.0)), axis=-1)
    raised = jnp.exp(chosen)
    return (normed, raised / jnp.sum(raised, axis=-1, keepdims=True))


def cp_pieces(x, n_cp):
    pieces = [x]
    for shift in range(1, n_cp):
        perm = [(i, (i + shift) % n_cp) for i in range(n_cp)]
        pieces.append(lax.ppermute(x, "cp", perm))
    return pieces


def expert_rows(received, full_gate, full_up, full_down):
    width = received.shape[-1]
    flat_rows = received.reshape(-1, width)
    gate_act = jnp.dot(flat_rows, full_gate[0], preferred_element_type=jnp.float32)
    up_act = jnp.dot(flat_rows, full_up[0], preferred_element_type=jnp.float32)
    hidden_act = (jax.nn.silu(gate_act) * up_act).astype(jnp.bfloat16)
    served = jnp.einsum(
        "rf,df->rd", hidden_act, full_down[0], preferred_element_type=jnp.float32
    ).astype(jnp.bfloat16)
    return served.reshape(received.shape)


def shards(
    query,
    keys,
    values,
    segment_ids,
    query_norm_gain,
    key_norm_gain,
    out_weight,
    residual,
    norm_gain,
    router_weight,
    expert_ids,
    expert_gate,
    expert_up,
    expert_down,
    *,
    n_cp,
    n_tp,
    n_ep,
):
    packs = query.shape[0]
    row_count = query.shape[1]
    head_count = query.shape[2] // HEAD_WIDTH
    width = residual.shape[2]
    experts = router_weight.shape[1]
    top_count = expert_ids.shape[2]
    score_scale = HEAD_WIDTH ** (-0.5)

    query_rows_normed = root_mean_scale(
        query.astype(jnp.float32).reshape(packs, row_count, head_count, HEAD_WIDTH), query_norm_gain
    ).astype(jnp.bfloat16)
    key_rows_normed = root_mean_scale(keys.astype(jnp.float32), key_norm_gain).astype(jnp.bfloat16)
    key_value = jnp.concatenate([key_rows_normed, values], axis=-1)
    kv_all = jnp.concatenate(cp_pieces(key_value, n_cp), axis=1)
    doc_all = jnp.concatenate(cp_pieces(segment_ids, n_cp), axis=1)
    key_piece = kv_all[..., :HEAD_WIDTH]
    value_piece = kv_all[..., HEAD_WIDTH:]
    scores = (
        jnp.einsum(
            "pshd,pnd->phsn", query_rows_normed, key_piece, preferred_element_type=jnp.float32
        )
        * score_scale
    )
    same_doc = segment_ids[:, :, None] == doc_all[:, None, :]
    probs = jnp.where(same_doc[:, None], jnp.exp(scores), jnp.float32(0.0))
    denom = jnp.sum(probs, axis=-1)
    probs_b = probs.astype(jnp.bfloat16)
    summed = jnp.einsum("phsn,pnd->pshd", probs_b, value_piece, preferred_element_type=jnp.float32)
    attn = (
        (summed / jnp.transpose(denom, (0, 2, 1))[:, :, :, None])
        .astype(jnp.bfloat16)
        .reshape(packs * row_count, head_count * HEAD_WIDTH)
    )
    share = row_count // n_tp
    tp_index = lax.axis_index("tp")
    ep_index = lax.axis_index("ep")
    cp_index = lax.axis_index("cp")
    cap = capacity(share, top_count, experts)
    attn_pieces = cp_pieces(attn, n_cp)
    received_blocks = []
    for j, piece in enumerate(attn_pieces):
        if j > 0:
            piece, received_blocks[0] = lax.optimization_barrier((piece, received_blocks[0]))
        block = jnp.dot(piece, out_weight, preferred_element_type=jnp.float32).reshape(
            packs, row_count, out_weight.shape[1]
        )
        summed = lax.psum_scatter(
            block.astype(jnp.bfloat16), "tp", scatter_dimension=1, tiled=True
        )
        if j > 0:
            summed = lax.ppermute(summed, "cp", [(i, (i - j) % n_cp) for i in range(n_cp)])
        received_blocks.append(summed)
    blocks = jnp.stack(received_blocks, axis=2).astype(jnp.float32)
    source_block = (jnp.arange(n_cp, dtype=jnp.int32) - cp_index) % n_cp
    picks_block = source_block[:, None] == jnp.arange(n_cp, dtype=jnp.int32)[None, :]
    projected = jnp.sum(
        jnp.where(picks_block[None, None, :, :, None], blocks[:, :, None, :, :], jnp.float32(0.0)),
        axis=3,
    ).reshape(packs, share, width)
    first_row = tp_index * share
    state = lax.dynamic_slice_in_dim(residual, first_row, share, 1).astype(jnp.float32) + projected
    local_ids = lax.dynamic_slice_in_dim(expert_ids, first_row, share, 1).reshape(
        packs * share, top_count
    )
    home_rows = packs * share
    normed = root_mean_scale(state.reshape(home_rows, width), norm_gain).astype(jnp.bfloat16)

    attn_pieces, expert_gate, expert_up, expert_down = lax.optimization_barrier(
        (attn_pieces, expert_gate, expert_up, expert_down)
    )
    gate_pieces = cp_pieces(expert_gate, n_cp)
    normed, gate_pieces = lax.optimization_barrier((normed, gate_pieces))
    up_down = jnp.concatenate([expert_up, expert_down], axis=2)
    gate_pieces, up_down = lax.optimization_barrier((gate_pieces, up_down))
    up_down_pieces = cp_pieces(up_down, n_cp)

    lanes = 128
    cap2 = n_ep * cap
    n_slots = n_tp * cap2
    gathered = n_ep * share
    row_iota = jnp.arange(gathered, dtype=jnp.int32)
    earlier = (row_iota[:, None] > row_iota[None, :]).astype(jnp.bfloat16)
    contract = (((0,), (0,)), ((), ()))
    mixtures = []
    for chunk in range(packs):
        rows = normed[chunk * share : (chunk + 1) * share]
        ids = local_ids[chunk * share : (chunk + 1) * share]
        if chunk > 0:
            rows, ids, _ = lax.optimization_barrier((rows, ids, buffer))
        id_lanes = jnp.pad(ids.astype(jnp.bfloat16), ((0, 0), (0, lanes - top_count)))
        rows_all = lax.all_gather(
            jnp.concatenate([rows, id_lanes], axis=1), "ep", axis=0, tiled=True
        )
        normed_all = rows_all[:, :width]
        ids_all = rows_all[:, width : width + top_count].astype(jnp.int32)
        logits = jnp.dot(normed_all, router_weight, preferred_element_type=jnp.float32)
        picks = ids_all[:, :, None] == jnp.arange(experts, dtype=jnp.int32)[None, None, :]
        raised = jnp.exp(
            jnp.sum(jnp.where(picks, logits[:, None, :], jnp.float32(0.0)), axis=-1)
        )
        gates_all = raised / jnp.sum(raised, axis=-1, keepdims=True)
        mine = (ids_all % n_ep) == ep_index
        dest = ids_all // n_ep
        named = jnp.stack(
            [jnp.any(mine & (dest == j), axis=1) for j in range(n_tp)], axis=1
        ).astype(jnp.bfloat16)
        rank = jnp.dot(earlier, named, preferred_element_type=jnp.float32).astype(jnp.int32)
        rank_of = jnp.sum(
            jnp.where(dest[:, :, None] == jnp.arange(n_tp, dtype=jnp.int32)[None, None, :],
                      rank[:, None, :], 0),
            axis=-1,
        )
        target = jnp.where(mine, dest * cap2 + rank_of, jnp.int32(-1)).T
        if chunk == 0:
            full_gate = jnp.concatenate(gate_pieces, axis=2)
        hit = target[:, None, :] == jnp.arange(n_slots, dtype=jnp.int32)[None, :, None]
        select = jnp.any(hit, axis=0).astype(jnp.bfloat16)
        weight = jnp.sum(jnp.where(hit, gates_all.T[:, None, :], jnp.float32(0.0)), axis=0)

        buffer = jnp.dot(select, normed_all, preferred_element_type=jnp.float32).astype(
            jnp.bfloat16
        )
        received = lax.all_to_all(
            buffer.reshape(n_tp, cap2, width), "tp", split_axis=0, concat_axis=0, tiled=True
        )
        if chunk == 0:
            received, up_down_pieces = lax.optimization_barrier((received, up_down_pieces))
            units = expert_up.shape[2]
            full_up = jnp.concatenate([p[:, :, :units] for p in up_down_pieces], axis=2)
            full_down = jnp.concatenate([p[:, :, units:] for p in up_down_pieces], axis=2)
        served = expert_rows(received, full_gate, full_up, full_down)
        back = lax.all_to_all(served, "tp", split_axis=0, concat_axis=0, tiled=True).reshape(
            n_slots, width
        )

        weight_hi = weight.astype(jnp.bfloat16)
        weight_lo = (weight - weight_hi.astype(jnp.float32)).astype(jnp.bfloat16)
        partial = lax.dot_general(
            weight_hi, back, contract, preferred_element_type=jnp.float32
        ) + lax.dot_general(weight_lo, back, contract, preferred_element_type=jnp.float32)
        mixtures.append(
            lax.psum_scatter(
                partial.astype(jnp.bfloat16).reshape(n_ep, share, width),
                "ep",
                scatter_dimension=0,
                tiled=True,
            )
        )
    mixture = jnp.concatenate(mixtures, axis=0).astype(jnp.float32)
    layer_out = (state + mixture).astype(jnp.bfloat16)
    return layer_out


def solution(mesh):
    body = functools.partial(
        shards, n_cp=mesh.shape["cp"], n_tp=mesh.shape["tp"], n_ep=mesh.shape["ep"]
    )
    return jax.shard_map(
        body,
        mesh=mesh,
        in_specs=(
            P("ep", "cp", "tp"),
            P("ep", "cp", "tp"),
            P("ep", "cp", "tp"),
            P("ep", "cp"),
            P(),
            P(),
            P("tp", "cp"),
            P("ep", "cp", None),
            P(),
            P(),
            P("ep", "cp", None),
            P(("tp", "ep"), None, "cp"),
            P(("tp", "ep"), None, "cp"),
            P(("tp", "ep"), None, "cp"),
        ),
        out_specs=P("ep", ("cp", "tp"), None),
        check_vma=False,
    )
```

```python
import functools

import jax
import jax.numpy as jnp
from jax import lax
from jax.sharding import PartitionSpec as P

HEAD_WIDTH = 128


def root_mean_scale(entries, gain):
    mean_sq = jnp.mean(entries * entries, axis=-1, keepdims=True)
    return entries * lax.rsqrt(mean_sq + 1e-06) * gain


def capacity(share, top_count, experts):
    return min(
        share, max(2, share * top_count // experts + max(1, share * top_count // (8 * experts)))
    )


def slot_numbers(ids, experts):
    flat_ids = ids.reshape(-1)
    table = (flat_ids[:, None] == jnp.arange(experts, dtype=jnp.int32)[None, :]).astype(jnp.int32)
    before = jnp.cumsum(table, axis=0) - table
    return jnp.sum(before * table, axis=1).reshape(ids.shape)


def route(state, ids, norm_gain, router_weight):
    normed = root_mean_scale(state, norm_gain).astype(jnp.bfloat16)
    logits = jnp.dot(normed, router_weight, preferred_element_type=jnp.float32)
    experts = router_weight.shape[1]
    picks = ids[:, :, None] == jnp.arange(experts, dtype=jnp.int32)[None, None, :]
    chosen = jnp.sum(jnp.where(picks, logits[:, None, :], jnp.float32(0.0)), axis=-1)
    raised = jnp.exp(chosen)
    return (normed, raised / jnp.sum(raised, axis=-1, keepdims=True))


def cp_pieces(x, n_cp):
    pieces = [x]
    for shift in range(1, n_cp):
        perm = [(i, (i + shift) % n_cp) for i in range(n_cp)]
        pieces.append(lax.ppermute(x, "cp", perm))
    return pieces


def expert_rows(received, full_gate, full_up, full_down):
    width = received.shape[-1]
    flat_rows = received.reshape(-1, width)
    gate_act = jnp.dot(flat_rows, full_gate[0], preferred_element_type=jnp.float32)
    up_act = jnp.dot(flat_rows, full_up[0], preferred_element_type=jnp.float32)
    hidden_act = (jax.nn.silu(gate_act) * up_act).astype(jnp.bfloat16)
    served = jnp.einsum(
        "rf,df->rd", hidden_act, full_down[0], preferred_element_type=jnp.float32
    ).astype(jnp.bfloat16)
    return served.reshape(received.shape)


def shards(
    query,
    keys,
    values,
    segment_ids,
    query_norm_gain,
    key_norm_gain,
    out_weight,
    residual,
    norm_gain,
    router_weight,
    expert_ids,
    expert_gate,
    expert_up,
    expert_down,
    *,
    n_cp,
    n_tp,
    n_ep,
):
    packs = query.shape[0]
    row_count = query.shape[1]
    head_count = query.shape[2] // HEAD_WIDTH
    width = residual.shape[2]
    experts = router_weight.shape[1]
    top_count = expert_ids.shape[2]
    score_scale = HEAD_WIDTH ** (-0.5)

    query_rows_normed = root_mean_scale(
        query.astype(jnp.float32).reshape(packs, row_count, head_count, HEAD_WIDTH), query_norm_gain
    ).astype(jnp.bfloat16)
    key_rows_normed = root_mean_scale(keys.astype(jnp.float32), key_norm_gain).astype(jnp.bfloat16)
    key_value = jnp.concatenate([key_rows_normed, values], axis=-1)
    kv_all = jnp.concatenate(cp_pieces(key_value, n_cp), axis=1)
    doc_all = jnp.concatenate(cp_pieces(segment_ids, n_cp), axis=1)
    key_piece = kv_all[..., :HEAD_WIDTH]
    value_piece = kv_all[..., HEAD_WIDTH:]
    scores = (
        jnp.einsum(
            "pshd,pnd->phsn", query_rows_normed, key_piece, preferred_element_type=jnp.float32
        )
        * score_scale
    )
    same_doc = segment_ids[:, :, None] == doc_all[:, None, :]
    probs = jnp.where(same_doc[:, None], jnp.exp(scores), jnp.float32(0.0))
    denom = jnp.sum(probs, axis=-1)
    probs_b = probs.astype(jnp.bfloat16)
    summed = jnp.einsum("phsn,pnd->pshd", probs_b, value_piece, preferred_element_type=jnp.float32)
    attn = (
        (summed / jnp.transpose(denom, (0, 2, 1))[:, :, :, None])
        .astype(jnp.bfloat16)
        .reshape(packs * row_count, head_count * HEAD_WIDTH)
    )
    share = row_count // n_tp
    tp_index = lax.axis_index("tp")
    ep_index = lax.axis_index("ep")
    cp_index = lax.axis_index("cp")
    cap = capacity(share, top_count, experts)
    attn_pieces = cp_pieces(attn, n_cp)
    received_blocks = []
    for j, piece in enumerate(attn_pieces):
        if j > 0:
            piece, received_blocks[0] = lax.optimization_barrier((piece, received_blocks[0]))
        block = jnp.dot(piece, out_weight, preferred_element_type=jnp.float32).reshape(
            packs, row_count, out_weight.shape[1]
        )
        summed = lax.psum_scatter(
            block.astype(jnp.bfloat16), "tp", scatter_dimension=1, tiled=True
        )
        if j > 0:
            summed = lax.ppermute(summed, "cp", [(i, (i - j) % n_cp) for i in range(n_cp)])
        received_blocks.append(summed)
    blocks = jnp.stack(received_blocks, axis=2).astype(jnp.float32)
    source_block = (jnp.arange(n_cp, dtype=jnp.int32) - cp_index) % n_cp
    picks_block = source_block[:, None] == jnp.arange(n_cp, dtype=jnp.int32)[None, :]
    projected = jnp.sum(
        jnp.where(picks_block[None, None, :, :, None], blocks[:, :, None, :, :], jnp.float32(0.0)),
        axis=3,
    ).reshape(packs, share, width)
    first_row = tp_index * share
    state = lax.dynamic_slice_in_dim(residual, first_row, share, 1).astype(jnp.float32) + projected
    local_ids = lax.dynamic_slice_in_dim(expert_ids, first_row, share, 1).reshape(
        packs * share, top_count
    )
    home_rows = packs * share
    normed = root_mean_scale(state.reshape(home_rows, width), norm_gain).astype(jnp.bfloat16)

    attn_pieces, expert_gate, expert_up, expert_down = lax.optimization_barrier(
        (attn_pieces, expert_gate, expert_up, expert_down)
    )
    gate_pieces = cp_pieces(expert_gate, n_cp)
    normed, gate_pieces = lax.optimization_barrier((normed, gate_pieces))
    up_down = jnp.concatenate([expert_up, expert_down], axis=2)
    gate_pieces, up_down = lax.optimization_barrier((gate_pieces, up_down))
    up_down_pieces = cp_pieces(up_down, n_cp)

    lanes = 128
    cap2 = n_ep * cap
    n_slots = n_tp * cap2
    gathered = n_ep * share
    row_iota = jnp.arange(gathered, dtype=jnp.int32)
    earlier = (row_iota[:, None] > row_iota[None, :]).astype(jnp.bfloat16)
    contract = (((0,), (0,)), ((), ()))
    mixtures = []
    for chunk in range(packs):
        rows = normed[chunk * share : (chunk + 1) * share]
        ids = local_ids[chunk * share : (chunk + 1) * share]
        if chunk > 0:
            rows, ids, _ = lax.optimization_barrier((rows, ids, buffer))
        id_lanes = jnp.pad(ids.astype(jnp.bfloat16), ((0, 0), (0, lanes - top_count)))
        rows_all = lax.all_gather(
            jnp.concatenate([rows, id_lanes], axis=1), "ep", axis=0, tiled=True
        )
        normed_all = rows_all[:, :width]
        ids_all = rows_all[:, width : width + top_count].astype(jnp.int32)
        logits = jnp.dot(normed_all, router_weight, preferred_element_type=jnp.float32)
        picks = ids_all[:, :, None] == jnp.arange(experts, dtype=jnp.int32)[None, None, :]
        raised = jnp.exp(
            jnp.sum(jnp.where(picks, logits[:, None, :], jnp.float32(0.0)), axis=-1)
        )
        gates_all = raised / jnp.sum(raised, axis=-1, keepdims=True)
        mine = (ids_all % n_ep) == ep_index
        dest = ids_all // n_ep
        named = jnp.stack(
            [jnp.any(mine & (dest == j), axis=1) for j in range(n_tp)], axis=1
        ).astype(jnp.bfloat16)
        rank = jnp.dot(earlier, named, preferred_element_type=jnp.float32).astype(jnp.int32)
        rank_of = jnp.sum(
            jnp.where(dest[:, :, None] == jnp.arange(n_tp, dtype=jnp.int32)[None, None, :],
                      rank[:, None, :], 0),
            axis=-1,
        )
        target = jnp.where(mine, dest * cap2 + rank_of, jnp.int32(-1)).T
        if chunk == 0:
            full_gate = jnp.concatenate(gate_pieces, axis=2)
        hit = target[:, None, :] == jnp.arange(n_slots, dtype=jnp.int32)[None, :, None]
        select = jnp.any(hit, axis=0).astype(jnp.bfloat16)
        weight = jnp.sum(jnp.where(hit, gates_all.T[:, None, :], jnp.float32(0.0)), axis=0)

        buffer = jnp.dot(select, normed_all, preferred_element_type=jnp.float32).astype(
            jnp.bfloat16
        )
        received = lax.all_to_all(
            buffer.reshape(n_tp, cap2, width), "tp", split_axis=0, concat_axis=0, tiled=True
        )
        if chunk == 0:
            received, up_down_pieces = lax.optimization_barrier((received, up_down_pieces))
            units = expert_up.shape[2]
            full_up = jnp.concatenate([p[:, :, :units] for p in up_down_pieces], axis=2)
            full_down = jnp.concatenate([p[:, :, units:] for p in up_down_pieces], axis=2)
        served = expert_rows(received, full_gate, full_up, full_down)
        back = lax.all_to_all(served, "tp", split_axis=0, concat_axis=0, tiled=True).reshape(
            n_slots, width
        )

        partial = lax.dot_general(
            weight,
            back.astype(jnp.float32),
            contract,
            precision=lax.Precision.HIGHEST,
            preferred_element_type=jnp.float32,
        )
        mixtures.append(
            lax.psum_scatter(
                partial.astype(jnp.bfloat16).reshape(n_ep, share, width),
                "ep",
                scatter_dimension=0,
                tiled=True,
            )
        )
    mixture = jnp.concatenate(mixtures, axis=0).astype(jnp.float32)
    layer_out = (state + mixture).astype(jnp.bfloat16)
    return layer_out


def solution(mesh):
    body = functools.partial(
        shards, n_cp=mesh.shape["cp"], n_tp=mesh.shape["tp"], n_ep=mesh.shape["ep"]
    )
    return jax.shard_map(
        body,
        mesh=mesh,
        in_specs=(
            P("ep", "cp", "tp"),
            P("ep", "cp", "tp"),
            P("ep", "cp", "tp"),
            P("ep", "cp"),
            P(),
            P(),
            P("tp", "cp"),
            P("ep", "cp", None),
            P(),
            P(),
            P("ep", "cp", None),
            P(("tp", "ep"), None, "cp"),
            P(("tp", "ep"), None, "cp"),
            P(("tp", "ep"), None, "cp"),
        ),
        out_specs=P("ep", ("cp", "tp"), None),
        check_vma=False,
    )
```

```python
import functools

import jax
import jax.numpy as jnp
from jax import lax
from jax.sharding import PartitionSpec as P

HEAD_WIDTH = 128


def root_mean_scale(entries, gain):
    mean_sq = jnp.mean(entries * entries, axis=-1, keepdims=True)
    return entries * lax.rsqrt(mean_sq + 1e-06) * gain


def capacity(share, top_count, experts):
    return min(
        share, max(2, share * top_count // experts + max(1, share * top_count // (8 * experts)))
    )


def slot_numbers(ids, experts):
    flat_ids = ids.reshape(-1)
    table = (flat_ids[:, None] == jnp.arange(experts, dtype=jnp.int32)[None, :]).astype(jnp.int32)
    before = jnp.cumsum(table, axis=0) - table
    return jnp.sum(before * table, axis=1).reshape(ids.shape)


def route(state, ids, norm_gain, router_weight):
    normed = root_mean_scale(state, norm_gain).astype(jnp.bfloat16)
    logits = jnp.dot(normed, router_weight, preferred_element_type=jnp.float32)
    experts = router_weight.shape[1]
    picks = ids[:, :, None] == jnp.arange(experts, dtype=jnp.int32)[None, None, :]
    chosen = jnp.sum(jnp.where(picks, logits[:, None, :], jnp.float32(0.0)), axis=-1)
    raised = jnp.exp(chosen)
    return (normed, raised / jnp.sum(raised, axis=-1, keepdims=True))


def cp_pieces(x, n_cp):
    pieces = [x]
    for shift in range(1, n_cp):
        perm = [(i, (i + shift) % n_cp) for i in range(n_cp)]
        pieces.append(lax.ppermute(x, "cp", perm))
    return pieces


def expert_rows(received, full_gate, full_up, full_down):
    width = received.shape[-1]
    flat_rows = received.reshape(-1, width)
    gate_act = jnp.dot(flat_rows, full_gate[0], preferred_element_type=jnp.float32)
    up_act = jnp.dot(flat_rows, full_up[0], preferred_element_type=jnp.float32)
    hidden_act = (jax.nn.silu(gate_act) * up_act).astype(jnp.bfloat16)
    served = jnp.einsum(
        "rf,df->rd", hidden_act, full_down[0], preferred_element_type=jnp.float32
    ).astype(jnp.bfloat16)
    return served.reshape(received.shape)


def shards(
    query,
    keys,
    values,
    segment_ids,
    query_norm_gain,
    key_norm_gain,
    out_weight,
    residual,
    norm_gain,
    router_weight,
    expert_ids,
    expert_gate,
    expert_up,
    expert_down,
    *,
    n_cp,
    n_tp,
    n_ep,
):
    packs = query.shape[0]
    row_count = query.shape[1]
    head_count = query.shape[2] // HEAD_WIDTH
    width = residual.shape[2]
    experts = router_weight.shape[1]
    top_count = expert_ids.shape[2]
    score_scale = HEAD_WIDTH ** (-0.5)

    query_pieces = cp_pieces(query, n_cp)
    key_rows_normed = root_mean_scale(keys.astype(jnp.float32), key_norm_gain).astype(jnp.bfloat16)
    key_value = jnp.concatenate([key_rows_normed, values], axis=-1)
    doc_pieces = cp_pieces(segment_ids, n_cp)
    kv_all = jnp.concatenate(cp_pieces(key_value, n_cp), axis=1)
    doc_all = jnp.concatenate(doc_pieces, axis=1)
    key_piece = kv_all[..., :HEAD_WIDTH]
    value_piece = kv_all[..., HEAD_WIDTH:]

    def attention(query_rows, docs):
        query_rows_normed = root_mean_scale(
            query_rows.astype(jnp.float32).reshape(packs, row_count, head_count, HEAD_WIDTH),
            query_norm_gain,
        ).astype(jnp.bfloat16)
        scores = (
            jnp.einsum(
                "pshd,pnd->phsn", query_rows_normed, key_piece, preferred_element_type=jnp.float32
            )
            * score_scale
        )
        same_doc = docs[:, :, None] == doc_all[:, None, :]
        probs = jnp.where(same_doc[:, None], jnp.exp(scores), jnp.float32(0.0))
        denom = jnp.sum(probs, axis=-1)
        probs_b = probs.astype(jnp.bfloat16)
        summed = jnp.einsum(
            "phsn,pnd->pshd", probs_b, value_piece, preferred_element_type=jnp.float32
        )
        return (
            (summed / jnp.transpose(denom, (0, 2, 1))[:, :, :, None])
            .astype(jnp.bfloat16)
            .reshape(packs * row_count, head_count * HEAD_WIDTH)
        )

    share = row_count // n_tp
    tp_index = lax.axis_index("tp")
    ep_index = lax.axis_index("ep")
    cp_index = lax.axis_index("cp")
    cap = capacity(share, top_count, experts)
    received_blocks = []
    for j in range(n_cp):
        piece = attention(query_pieces[j], doc_pieces[j])
        block = jnp.dot(piece, out_weight, preferred_element_type=jnp.float32).reshape(
            packs, row_count, out_weight.shape[1]
        )
        summed = lax.psum_scatter(
            block.astype(jnp.bfloat16), "tp", scatter_dimension=1, tiled=True
        )
        if j > 0:
            summed = lax.ppermute(summed, "cp", [(i, (i - j) % n_cp) for i in range(n_cp)])
        received_blocks.append(summed)
    blocks = jnp.stack(received_blocks, axis=2).astype(jnp.float32)
    source_block = (jnp.arange(n_cp, dtype=jnp.int32) - cp_index) % n_cp
    picks_block = source_block[:, None] == jnp.arange(n_cp, dtype=jnp.int32)[None, :]
    projected = jnp.sum(
        jnp.where(picks_block[None, None, :, :, None], blocks[:, :, None, :, :], jnp.float32(0.0)),
        axis=3,
    ).reshape(packs, share, width)
    first_row = tp_index * share
    state = lax.dynamic_slice_in_dim(residual, first_row, share, 1).astype(jnp.float32) + projected
    local_ids = lax.dynamic_slice_in_dim(expert_ids, first_row, share, 1).reshape(
        packs * share, top_count
    )
    home_rows = packs * share
    normed = root_mean_scale(state.reshape(home_rows, width), norm_gain).astype(jnp.bfloat16)

    query_pieces, expert_gate, expert_up, expert_down = lax.optimization_barrier(
        (query_pieces, expert_gate, expert_up, expert_down)
    )
    gate_pieces = cp_pieces(expert_gate, n_cp)
    normed, gate_pieces = lax.optimization_barrier((normed, gate_pieces))
    up_down = jnp.concatenate([expert_up, expert_down], axis=2)
    gate_pieces, up_down = lax.optimization_barrier((gate_pieces, up_down))
    up_down_pieces = cp_pieces(up_down, n_cp)

    lanes = 128
    cap2 = n_ep * cap
    n_slots = n_tp * cap2
    gathered = n_ep * share
    row_iota = jnp.arange(gathered, dtype=jnp.int32)
    earlier = (row_iota[:, None] > row_iota[None, :]).astype(jnp.bfloat16)
    contract = (((0,), (0,)), ((), ()))
    mixtures = []
    for chunk in range(packs):
        rows = normed[chunk * share : (chunk + 1) * share]
        ids = local_ids[chunk * share : (chunk + 1) * share]
        if chunk > 0:
            rows, ids, _ = lax.optimization_barrier((rows, ids, buffer))
        id_lanes = jnp.pad(ids.astype(jnp.bfloat16), ((0, 0), (0, lanes - top_count)))
        rows_all = lax.all_gather(
            jnp.concatenate([rows, id_lanes], axis=1), "ep", axis=0, tiled=True
        )
        normed_all = rows_all[:, :width]
        ids_all = rows_all[:, width : width + top_count].astype(jnp.int32)
        logits = jnp.dot(normed_all, router_weight, preferred_element_type=jnp.float32)
        picks = ids_all[:, :, None] == jnp.arange(experts, dtype=jnp.int32)[None, None, :]
        raised = jnp.exp(
            jnp.sum(jnp.where(picks, logits[:, None, :], jnp.float32(0.0)), axis=-1)
        )
        gates_all = raised / jnp.sum(raised, axis=-1, keepdims=True)
        mine = (ids_all % n_ep) == ep_index
        dest = ids_all // n_ep
        named = jnp.stack(
            [jnp.any(mine & (dest == j), axis=1) for j in range(n_tp)], axis=1
        ).astype(jnp.bfloat16)
        rank = jnp.dot(earlier, named, preferred_element_type=jnp.float32).astype(jnp.int32)
        rank_of = jnp.sum(
            jnp.where(dest[:, :, None] == jnp.arange(n_tp, dtype=jnp.int32)[None, None, :],
                      rank[:, None, :], 0),
            axis=-1,
        )
        target = jnp.where(mine, dest * cap2 + rank_of, jnp.int32(-1)).T
        if chunk == 0:
            full_gate = jnp.concatenate(gate_pieces, axis=2)
        hit = target[:, None, :] == jnp.arange(n_slots, dtype=jnp.int32)[None, :, None]
        select = jnp.any(hit, axis=0).astype(jnp.bfloat16)
        weight = jnp.sum(jnp.where(hit, gates_all.T[:, None, :], jnp.float32(0.0)), axis=0)

        buffer = jnp.dot(select, normed_all, preferred_element_type=jnp.float32).astype(
            jnp.bfloat16
        )
        received = lax.all_to_all(
            buffer.reshape(n_tp, cap2, width), "tp", split_axis=0, concat_axis=0, tiled=True
        )
        if chunk == 0:
            received, up_down_pieces = lax.optimization_barrier((received, up_down_pieces))
            units = expert_up.shape[2]
            full_up = jnp.concatenate([p[:, :, :units] for p in up_down_pieces], axis=2)
            full_down = jnp.concatenate([p[:, :, units:] for p in up_down_pieces], axis=2)
        served = expert_rows(received, full_gate, full_up, full_down)
        back = lax.all_to_all(served, "tp", split_axis=0, concat_axis=0, tiled=True).reshape(
            n_slots, width
        )

        weight_hi = weight.astype(jnp.bfloat16)
        weight_lo = (weight - weight_hi.astype(jnp.float32)).astype(jnp.bfloat16)
        partial = lax.dot_general(
            weight_hi, back, contract, preferred_element_type=jnp.float32
        ) + lax.dot_general(weight_lo, back, contract, preferred_element_type=jnp.float32)
        mixtures.append(
            lax.psum_scatter(
                partial.astype(jnp.bfloat16).reshape(n_ep, share, width),
                "ep",
                scatter_dimension=0,
                tiled=True,
            )
        )
    mixture = jnp.concatenate(mixtures, axis=0).astype(jnp.float32)
    layer_out = (state + mixture).astype(jnp.bfloat16)
    return layer_out


def solution(mesh):
    body = functools.partial(
        shards, n_cp=mesh.shape["cp"], n_tp=mesh.shape["tp"], n_ep=mesh.shape["ep"]
    )
    return jax.shard_map(
        body,
        mesh=mesh,
        in_specs=(
            P("ep", "cp", "tp"),
            P("ep", "cp", "tp"),
            P("ep", "cp", "tp"),
            P("ep", "cp"),
            P(),
            P(),
            P("tp", "cp"),
            P("ep", "cp", None),
            P(),
            P(),
            P("ep", "cp", None),
            P(("tp", "ep"), None, "cp"),
            P(("tp", "ep"), None, "cp"),
            P(("tp", "ep"), None, "cp"),
        ),
        out_specs=P("ep", ("cp", "tp"), None),
        check_vma=False,
    )
```

```python
import functools

import jax
import jax.numpy as jnp
from jax import lax
from jax.sharding import PartitionSpec as P

HEAD_WIDTH = 128


def root_mean_scale(entries, gain):
    mean_sq = jnp.mean(entries * entries, axis=-1, keepdims=True)
    return entries * lax.rsqrt(mean_sq + 1e-06) * gain


def capacity(share, top_count, experts):
    return min(
        share, max(2, share * top_count // experts + max(1, share * top_count // (8 * experts)))
    )


def slot_numbers(ids, experts):
    flat_ids = ids.reshape(-1)
    table = (flat_ids[:, None] == jnp.arange(experts, dtype=jnp.int32)[None, :]).astype(jnp.int32)
    before = jnp.cumsum(table, axis=0) - table
    return jnp.sum(before * table, axis=1).reshape(ids.shape)


def route(state, ids, norm_gain, router_weight):
    normed = root_mean_scale(state, norm_gain).astype(jnp.bfloat16)
    logits = jnp.dot(normed, router_weight, preferred_element_type=jnp.float32)
    experts = router_weight.shape[1]
    picks = ids[:, :, None] == jnp.arange(experts, dtype=jnp.int32)[None, None, :]
    chosen = jnp.sum(jnp.where(picks, logits[:, None, :], jnp.float32(0.0)), axis=-1)
    raised = jnp.exp(chosen)
    return (normed, raised / jnp.sum(raised, axis=-1, keepdims=True))


def cp_pieces(x, n_cp):
    pieces = [x]
    for shift in range(1, n_cp):
        perm = [(i, (i + shift) % n_cp) for i in range(n_cp)]
        pieces.append(lax.ppermute(x, "cp", perm))
    return pieces


def expert_rows(received, full_gate, full_up, full_down):
    width = received.shape[-1]
    flat_rows = received.reshape(-1, width)
    gate_act = jnp.dot(flat_rows, full_gate[0], preferred_element_type=jnp.float32)
    up_act = jnp.dot(flat_rows, full_up[0], preferred_element_type=jnp.float32)
    hidden_act = (jax.nn.silu(gate_act) * up_act).astype(jnp.bfloat16)
    served = jnp.einsum(
        "rf,df->rd", hidden_act, full_down[0], preferred_element_type=jnp.float32
    ).astype(jnp.bfloat16)
    return served.reshape(received.shape)


def shards(
    query,
    keys,
    values,
    segment_ids,
    query_norm_gain,
    key_norm_gain,
    out_weight,
    residual,
    norm_gain,
    router_weight,
    expert_ids,
    expert_gate,
    expert_up,
    expert_down,
    *,
    n_cp,
    n_tp,
    n_ep,
):
    packs = query.shape[0]
    row_count = query.shape[1]
    head_count = query.shape[2] // HEAD_WIDTH
    width = residual.shape[2]
    experts = router_weight.shape[1]
    top_count = expert_ids.shape[2]
    score_scale = HEAD_WIDTH ** (-0.5)

    query_rows_normed = root_mean_scale(
        query.astype(jnp.float32).reshape(packs, row_count, head_count, HEAD_WIDTH), query_norm_gain
    ).astype(jnp.bfloat16)
    key_rows_normed = root_mean_scale(keys.astype(jnp.float32), key_norm_gain).astype(jnp.bfloat16)
    key_value = jnp.concatenate([key_rows_normed, values], axis=-1)
    kv_all = jnp.concatenate(cp_pieces(key_value, n_cp), axis=1)
    doc_all = jnp.concatenate(cp_pieces(segment_ids, n_cp), axis=1)
    key_piece = kv_all[..., :HEAD_WIDTH]
    value_piece = kv_all[..., HEAD_WIDTH:]
    scores = (
        jnp.einsum(
            "pshd,pnd->phsn", query_rows_normed, key_piece, preferred_element_type=jnp.float32
        )
        * score_scale
    )
    same_doc = segment_ids[:, :, None] == doc_all[:, None, :]
    probs = jnp.where(same_doc[:, None], jnp.exp(scores), jnp.float32(0.0))
    denom = jnp.sum(probs, axis=-1)
    probs_b = probs.astype(jnp.bfloat16)
    summed = jnp.einsum("phsn,pnd->pshd", probs_b, value_piece, preferred_element_type=jnp.float32)
    attn = (
        (summed / jnp.transpose(denom, (0, 2, 1))[:, :, :, None])
        .astype(jnp.bfloat16)
        .reshape(packs * row_count, head_count * HEAD_WIDTH)
    )
    share = row_count // n_tp
    tp_index = lax.axis_index("tp")
    ep_index = lax.axis_index("ep")
    cp_index = lax.axis_index("cp")
    cap = capacity(share, top_count, experts)
    attn_pieces = cp_pieces(attn, n_cp)
    received_blocks = []
    for j, piece in enumerate(attn_pieces):
        if j > 0:
            piece, received_blocks[0] = lax.optimization_barrier((piece, received_blocks[0]))
        block = jnp.dot(piece, out_weight, preferred_element_type=jnp.float32).reshape(
            packs, row_count, out_weight.shape[1]
        )
        summed = lax.psum_scatter(
            block.astype(jnp.bfloat16), "tp", scatter_dimension=1, tiled=True
        )
        if j > 0:
            summed = lax.ppermute(summed, "cp", [(i, (i - j) % n_cp) for i in range(n_cp)])
        received_blocks.append(summed)
    blocks = jnp.stack(received_blocks, axis=2).astype(jnp.float32)
    source_block = (jnp.arange(n_cp, dtype=jnp.int32) - cp_index) % n_cp
    picks_block = source_block[:, None] == jnp.arange(n_cp, dtype=jnp.int32)[None, :]
    projected = jnp.sum(
        jnp.where(picks_block[None, None, :, :, None], blocks[:, :, None, :, :], jnp.float32(0.0)),
        axis=3,
    ).reshape(packs, share, width)
    first_row = tp_index * share
    state = lax.dynamic_slice_in_dim(residual, first_row, share, 1).astype(jnp.float32) + projected
    local_ids = lax.dynamic_slice_in_dim(expert_ids, first_row, share, 1).reshape(
        packs * share, top_count
    )
    home_rows = packs * share
    normed = root_mean_scale(state.reshape(home_rows, width), norm_gain).astype(jnp.bfloat16)

    attn_pieces, expert_gate, expert_up, expert_down = lax.optimization_barrier(
        (attn_pieces, expert_gate, expert_up, expert_down)
    )
    gate_pieces = cp_pieces(expert_gate, n_cp)
    normed, gate_pieces = lax.optimization_barrier((normed, gate_pieces))
    up_down = jnp.concatenate([expert_up, expert_down], axis=2)
    gate_pieces, up_down = lax.optimization_barrier((gate_pieces, up_down))
    up_down_pieces = cp_pieces(up_down, n_cp)

    lanes = 128
    cap2 = n_ep * cap
    n_slots = n_tp * cap2
    gathered = n_ep * share
    row_iota = jnp.arange(gathered, dtype=jnp.int32)
    earlier = (row_iota[:, None] > row_iota[None, :]).astype(jnp.bfloat16)
    mixtures = []
    for chunk in range(packs):
        rows = normed[chunk * share : (chunk + 1) * share]
        ids = local_ids[chunk * share : (chunk + 1) * share]
        if chunk > 0:
            rows, ids, _ = lax.optimization_barrier((rows, ids, buffer))
        id_lanes = jnp.pad(ids.astype(jnp.bfloat16), ((0, 0), (0, lanes - top_count)))
        rows_all = lax.all_gather(
            jnp.concatenate([rows, id_lanes], axis=1), "ep", axis=0, tiled=True
        )
        normed_all = rows_all[:, :width]
        ids_all = rows_all[:, width : width + top_count].astype(jnp.int32)
        logits = jnp.dot(normed_all, router_weight, preferred_element_type=jnp.float32)
        picks = ids_all[:, :, None] == jnp.arange(experts, dtype=jnp.int32)[None, None, :]
        raised = jnp.exp(
            jnp.sum(jnp.where(picks, logits[:, None, :], jnp.float32(0.0)), axis=-1)
        )
        gates_all = raised / jnp.sum(raised, axis=-1, keepdims=True)
        mine = (ids_all % n_ep) == ep_index
        dest = ids_all // n_ep
        named = jnp.stack(
            [jnp.any(mine & (dest == j), axis=1) for j in range(n_tp)], axis=1
        ).astype(jnp.bfloat16)
        rank = jnp.dot(earlier, named, preferred_element_type=jnp.float32).astype(jnp.int32)
        rank_of = jnp.sum(
            jnp.where(dest[:, :, None] == jnp.arange(n_tp, dtype=jnp.int32)[None, None, :],
                      rank[:, None, :], 0),
            axis=-1,
        )
        target = jnp.where(mine, dest * cap2 + rank_of, jnp.int32(-1)).T
        if chunk == 0:
            full_gate = jnp.concatenate(gate_pieces, axis=2)
        hit = target[:, None, :] == jnp.arange(n_slots, dtype=jnp.int32)[None, :, None]
        select = jnp.any(hit, axis=0).astype(jnp.bfloat16)
        hit_by_token = target[:, :, None] == jnp.arange(n_slots, dtype=jnp.int32)[None, None, :]
        weight = jnp.sum(
            jnp.where(hit_by_token, gates_all.T[:, :, None], jnp.float32(0.0)), axis=0
        )

        buffer = jnp.dot(select, normed_all, preferred_element_type=jnp.float32).astype(
            jnp.bfloat16
        )
        received = lax.all_to_all(
            buffer.reshape(n_tp, cap2, width), "tp", split_axis=0, concat_axis=0, tiled=True
        )
        if chunk == 0:
            received, up_down_pieces = lax.optimization_barrier((received, up_down_pieces))
            units = expert_up.shape[2]
            full_up = jnp.concatenate([p[:, :, :units] for p in up_down_pieces], axis=2)
            full_down = jnp.concatenate([p[:, :, units:] for p in up_down_pieces], axis=2)
        served = expert_rows(received, full_gate, full_up, full_down)
        back = lax.all_to_all(served, "tp", split_axis=0, concat_axis=0, tiled=True).reshape(
            n_slots, width
        )

        weight_hi = weight.astype(jnp.bfloat16)
        weight_lo = (weight - weight_hi.astype(jnp.float32)).astype(jnp.bfloat16)
        partial = jnp.dot(weight_hi, back, preferred_element_type=jnp.float32) + jnp.dot(
            weight_lo, back, preferred_element_type=jnp.float32
        )
        mixtures.append(
            lax.psum_scatter(
                partial.astype(jnp.bfloat16).reshape(n_ep, share, width),
                "ep",
                scatter_dimension=0,
                tiled=True,
            )
        )
    mixture = jnp.concatenate(mixtures, axis=0).astype(jnp.float32)
    layer_out = (state + mixture).astype(jnp.bfloat16)
    return layer_out


def solution(mesh):
    body = functools.partial(
        shards, n_cp=mesh.shape["cp"], n_tp=mesh.shape["tp"], n_ep=mesh.shape["ep"]
    )
    return jax.shard_map(
        body,
        mesh=mesh,
        in_specs=(
            P("ep", "cp", "tp"),
            P("ep", "cp", "tp"),
            P("ep", "cp", "tp"),
            P("ep", "cp"),
            P(),
            P(),
            P("tp", "cp"),
            P("ep", "cp", None),
            P(),
            P(),
            P("ep", "cp", None),
            P(("tp", "ep"), None, "cp"),
            P(("tp", "ep"), None, "cp"),
            P(("tp", "ep"), None, "cp"),
        ),
        out_specs=P("ep", ("cp", "tp"), None),
        check_vma=False,
    )
```

```python
import functools

import jax
import jax.numpy as jnp
from jax import lax
from jax.sharding import PartitionSpec as P

HEAD_WIDTH = 128


def root_mean_scale(entries, gain):
    mean_sq = jnp.mean(entries * entries, axis=-1, keepdims=True)
    return entries * lax.rsqrt(mean_sq + 1e-06) * gain


def capacity(share, top_count, experts):
    return min(
        share, max(2, share * top_count // experts + max(1, share * top_count // (8 * experts)))
    )


def slot_numbers(ids, experts):
    flat_ids = ids.reshape(-1)
    table = (flat_ids[:, None] == jnp.arange(experts, dtype=jnp.int32)[None, :]).astype(jnp.int32)
    before = jnp.cumsum(table, axis=0) - table
    return jnp.sum(before * table, axis=1).reshape(ids.shape)


def route(state, ids, norm_gain, router_weight):
    normed = root_mean_scale(state, norm_gain).astype(jnp.bfloat16)
    logits = jnp.dot(normed, router_weight, preferred_element_type=jnp.float32)
    experts = router_weight.shape[1]
    picks = ids[:, :, None] == jnp.arange(experts, dtype=jnp.int32)[None, None, :]
    chosen = jnp.sum(jnp.where(picks, logits[:, None, :], jnp.float32(0.0)), axis=-1)
    raised = jnp.exp(chosen)
    return (normed, raised / jnp.sum(raised, axis=-1, keepdims=True))


def cp_pieces(x, n_cp):
    pieces = [x]
    for shift in range(1, n_cp):
        perm = [(i, (i + shift) % n_cp) for i in range(n_cp)]
        pieces.append(lax.ppermute(x, "cp", perm))
    return pieces


def expert_rows(received, full_gate, full_up, full_down):
    width = received.shape[-1]
    flat_rows = received.reshape(-1, width)
    gate_act = jnp.dot(flat_rows, full_gate[0], preferred_element_type=jnp.float32)
    up_act = jnp.dot(flat_rows, full_up[0], preferred_element_type=jnp.float32)
    hidden_act = (jax.nn.silu(gate_act) * up_act).astype(jnp.bfloat16)
    served = jnp.einsum(
        "rf,df->rd", hidden_act, full_down[0], preferred_element_type=jnp.float32
    ).astype(jnp.bfloat16)
    return served.reshape(received.shape)


def shards(
    query,
    keys,
    values,
    segment_ids,
    query_norm_gain,
    key_norm_gain,
    out_weight,
    residual,
    norm_gain,
    router_weight,
    expert_ids,
    expert_gate,
    expert_up,
    expert_down,
    *,
    n_cp,
    n_tp,
    n_ep,
):
    packs = query.shape[0]
    row_count = query.shape[1]
    head_count = query.shape[2] // HEAD_WIDTH
    width = residual.shape[2]
    experts = router_weight.shape[1]
    top_count = expert_ids.shape[2]
    score_scale = HEAD_WIDTH ** (-0.5)

    query_rows_normed = root_mean_scale(
        query.astype(jnp.float32).reshape(packs, row_count, head_count, HEAD_WIDTH), query_norm_gain
    ).astype(jnp.bfloat16)
    key_rows_normed = root_mean_scale(keys.astype(jnp.float32), key_norm_gain).astype(jnp.bfloat16)
    key_value = jnp.concatenate([key_rows_normed, values], axis=-1)
    kv_all = jnp.concatenate(cp_pieces(key_value, n_cp), axis=1)
    doc_all = jnp.concatenate(cp_pieces(segment_ids, n_cp), axis=1)
    key_piece = kv_all[..., :HEAD_WIDTH]
    value_piece = kv_all[..., HEAD_WIDTH:]
    scores = (
        jnp.einsum(
            "pshd,pnd->phsn", query_rows_normed, key_piece, preferred_element_type=jnp.float32
        )
        * score_scale
    )
    same_doc = segment_ids[:, :, None] == doc_all[:, None, :]
    probs = jnp.where(same_doc[:, None], jnp.exp(scores), jnp.float32(0.0))
    denom = jnp.sum(probs, axis=-1)
    probs_b = probs.astype(jnp.bfloat16)
    summed = jnp.einsum("phsn,pnd->pshd", probs_b, value_piece, preferred_element_type=jnp.float32)
    attn = (
        (summed / jnp.transpose(denom, (0, 2, 1))[:, :, :, None])
        .astype(jnp.bfloat16)
        .reshape(packs * row_count, head_count * HEAD_WIDTH)
    )
    share = row_count // n_tp
    tp_index = lax.axis_index("tp")
    ep_index = lax.axis_index("ep")
    cp_index = lax.axis_index("cp")
    cap = capacity(share, top_count, experts)
    attn_pieces = cp_pieces(attn, n_cp)
    received_blocks = []
    for j, piece in enumerate(attn_pieces):
        if j > 0:
            piece, received_blocks[0] = lax.optimization_barrier((piece, received_blocks[0]))
        block = jnp.dot(piece, out_weight, preferred_element_type=jnp.float32).reshape(
            packs, row_count, out_weight.shape[1]
        )
        summed = lax.psum_scatter(
            block.astype(jnp.bfloat16), "tp", scatter_dimension=1, tiled=True
        )
        if j > 0:
            summed = lax.ppermute(summed, "cp", [(i, (i - j) % n_cp) for i in range(n_cp)])
        received_blocks.append(summed)
    blocks = jnp.stack(received_blocks, axis=2).astype(jnp.float32)
    source_block = (jnp.arange(n_cp, dtype=jnp.int32) - cp_index) % n_cp
    picks_block = source_block[:, None] == jnp.arange(n_cp, dtype=jnp.int32)[None, :]
    projected = jnp.sum(
        jnp.where(picks_block[None, None, :, :, None], blocks[:, :, None, :, :], jnp.float32(0.0)),
        axis=3,
    ).reshape(packs, share, width)
    first_row = tp_index * share
    state = lax.dynamic_slice_in_dim(residual, first_row, share, 1).astype(jnp.float32) + projected
    local_ids = lax.dynamic_slice_in_dim(expert_ids, first_row, share, 1).reshape(
        packs * share, top_count
    )
    home_rows = packs * share
    normed = root_mean_scale(state.reshape(home_rows, width), norm_gain).astype(jnp.bfloat16)

    attn_pieces, expert_gate, expert_up, expert_down = lax.optimization_barrier(
        (attn_pieces, expert_gate, expert_up, expert_down)
    )
    gate_pieces = cp_pieces(expert_gate, n_cp)
    normed, gate_pieces = lax.optimization_barrier((normed, gate_pieces))
    up_down = jnp.concatenate([expert_up, expert_down], axis=2)
    gate_pieces, up_down = lax.optimization_barrier((gate_pieces, up_down))
    up_down_pieces = cp_pieces(up_down, n_cp)

    lanes = 128
    cap2 = n_ep * cap
    n_slots = n_tp * cap2
    gathered = n_ep * share
    row_iota = jnp.arange(gathered, dtype=jnp.int32)
    earlier = (row_iota[:, None] > row_iota[None, :]).astype(jnp.bfloat16)
    contract = (((0,), (0,)), ((), ()))
    id_lanes = jnp.pad(local_ids.astype(jnp.bfloat16), ((0, 0), (0, lanes - top_count)))
    rows_with_ids = jnp.concatenate([normed, id_lanes], axis=1)
    mixtures = []
    for chunk in range(packs):
        rows = rows_with_ids[chunk * share : (chunk + 1) * share]
        if chunk > 0:
            rows, _ = lax.optimization_barrier((rows, buffer))
        rows_all = lax.all_gather(rows, "ep", axis=0, tiled=True)
        normed_all = rows_all[:, :width]
        ids_all = rows_all[:, width : width + top_count].astype(jnp.int32)
        logits = jnp.dot(normed_all, router_weight, preferred_element_type=jnp.float32)
        picks = ids_all[:, :, None] == jnp.arange(experts, dtype=jnp.int32)[None, None, :]
        raised = jnp.exp(
            jnp.sum(jnp.where(picks, logits[:, None, :], jnp.float32(0.0)), axis=-1)
        )
        gates_all = raised / jnp.sum(raised, axis=-1, keepdims=True)
        mine = (ids_all % n_ep) == ep_index
        dest = ids_all // n_ep
        named = jnp.stack(
            [jnp.any(mine & (dest == j), axis=1) for j in range(n_tp)], axis=1
        ).astype(jnp.bfloat16)
        rank = jnp.dot(earlier, named, preferred_element_type=jnp.float32).astype(jnp.int32)
        rank_of = jnp.sum(
            jnp.where(dest[:, :, None] == jnp.arange(n_tp, dtype=jnp.int32)[None, None, :],
                      rank[:, None, :], 0),
            axis=-1,
        )
        target = jnp.where(mine, dest * cap2 + rank_of, jnp.int32(-1)).T
        if chunk == 0:
            full_gate = jnp.concatenate(gate_pieces, axis=2)
        hit = target[:, None, :] == jnp.arange(n_slots, dtype=jnp.int32)[None, :, None]
        select = jnp.any(hit, axis=0).astype(jnp.bfloat16)
        weight = jnp.sum(jnp.where(hit, gates_all.T[:, None, :], jnp.float32(0.0)), axis=0)

        buffer = jnp.dot(select, normed_all, preferred_element_type=jnp.float32).astype(
            jnp.bfloat16
        )
        received = lax.all_to_all(
            buffer.reshape(n_tp, cap2, width), "tp", split_axis=0, concat_axis=0, tiled=True
        )
        if chunk == 0:
            received, up_down_pieces = lax.optimization_barrier((received, up_down_pieces))
            units = expert_up.shape[2]
            full_up = jnp.concatenate([p[:, :, :units] for p in up_down_pieces], axis=2)
            full_down = jnp.concatenate([p[:, :, units:] for p in up_down_pieces], axis=2)
        served = expert_rows(received, full_gate, full_up, full_down)
        back = lax.all_to_all(served, "tp", split_axis=0, concat_axis=0, tiled=True).reshape(
            n_slots, width
        )

        weight_hi = weight.astype(jnp.bfloat16)
        weight_lo = (weight - weight_hi.astype(jnp.float32)).astype(jnp.bfloat16)
        partial = lax.dot_general(
            weight_hi, back, contract, preferred_element_type=jnp.float32
        ) + lax.dot_general(weight_lo, back, contract, preferred_element_type=jnp.float32)
        mixtures.append(
            lax.psum_scatter(
                partial.astype(jnp.bfloat16).reshape(n_ep, share, width),
                "ep",
                scatter_dimension=0,
                tiled=True,
            )
        )
    mixture = jnp.concatenate(mixtures, axis=0).astype(jnp.float32)
    layer_out = (state + mixture).astype(jnp.bfloat16)
    return layer_out


def solution(mesh):
    body = functools.partial(
        shards, n_cp=mesh.shape["cp"], n_tp=mesh.shape["tp"], n_ep=mesh.shape["ep"]
    )
    return jax.shard_map(
        body,
        mesh=mesh,
        in_specs=(
            P("ep", "cp", "tp"),
            P("ep", "cp", "tp"),
            P("ep", "cp", "tp"),
            P("ep", "cp"),
            P(),
            P(),
            P("tp", "cp"),
            P("ep", "cp", None),
            P(),
            P(),
            P("ep", "cp", None),
            P(("tp", "ep"), None, "cp"),
            P(("tp", "ep"), None, "cp"),
            P(("tp", "ep"), None, "cp"),
        ),
        out_specs=P("ep", ("cp", "tp"), None),
        check_vma=False,
    )
```

```python
import functools

import jax
import jax.numpy as jnp
from jax import lax
from jax.sharding import PartitionSpec as P

HEAD_WIDTH = 128


def root_mean_scale(entries, gain):
    mean_sq = jnp.mean(entries * entries, axis=-1, keepdims=True)
    return entries * lax.rsqrt(mean_sq + 1e-06) * gain


def capacity(share, top_count, experts):
    return min(
        share, max(2, share * top_count // experts + max(1, share * top_count // (8 * experts)))
    )


def slot_numbers(ids, experts):
    flat_ids = ids.reshape(-1)
    table = (flat_ids[:, None] == jnp.arange(experts, dtype=jnp.int32)[None, :]).astype(jnp.int32)
    before = jnp.cumsum(table, axis=0) - table
    return jnp.sum(before * table, axis=1).reshape(ids.shape)


def route(state, ids, norm_gain, router_weight):
    normed = root_mean_scale(state, norm_gain).astype(jnp.bfloat16)
    logits = jnp.dot(normed, router_weight, preferred_element_type=jnp.float32)
    experts = router_weight.shape[1]
    picks = ids[:, :, None] == jnp.arange(experts, dtype=jnp.int32)[None, None, :]
    chosen = jnp.sum(jnp.where(picks, logits[:, None, :], jnp.float32(0.0)), axis=-1)
    raised = jnp.exp(chosen)
    return (normed, raised / jnp.sum(raised, axis=-1, keepdims=True))


def cp_pieces(x, n_cp):
    pieces = [x]
    for shift in range(1, n_cp):
        perm = [(i, (i + shift) % n_cp) for i in range(n_cp)]
        pieces.append(lax.ppermute(x, "cp", perm))
    return pieces


def expert_rows(received, full_gate, full_up, full_down):
    width = received.shape[-1]
    flat_rows = received.reshape(-1, width)
    gate_act = jnp.dot(flat_rows, full_gate[0], preferred_element_type=jnp.float32)
    up_act = jnp.dot(flat_rows, full_up[0], preferred_element_type=jnp.float32)
    hidden_act = (jax.nn.silu(gate_act) * up_act).astype(jnp.bfloat16)
    served = jnp.einsum(
        "rf,df->rd", hidden_act, full_down[0], preferred_element_type=jnp.float32
    ).astype(jnp.bfloat16)
    return served.reshape(received.shape)


def shards(
    query,
    keys,
    values,
    segment_ids,
    query_norm_gain,
    key_norm_gain,
    out_weight,
    residual,
    norm_gain,
    router_weight,
    expert_ids,
    expert_gate,
    expert_up,
    expert_down,
    *,
    n_cp,
    n_tp,
    n_ep,
):
    packs = query.shape[0]
    row_count = query.shape[1]
    head_count = query.shape[2] // HEAD_WIDTH
    width = residual.shape[2]
    experts = router_weight.shape[1]
    top_count = expert_ids.shape[2]
    score_scale = HEAD_WIDTH ** (-0.5)

    query_rows_normed = root_mean_scale(
        query.astype(jnp.float32).reshape(packs, row_count, head_count, HEAD_WIDTH), query_norm_gain
    ).astype(jnp.bfloat16)
    key_rows_normed = root_mean_scale(keys.astype(jnp.float32), key_norm_gain).astype(jnp.bfloat16)
    key_value = jnp.concatenate([key_rows_normed, values], axis=-1)
    kv_all = jnp.concatenate(cp_pieces(key_value, n_cp), axis=1)
    doc_all = jnp.concatenate(cp_pieces(segment_ids, n_cp), axis=1)
    key_piece = kv_all[..., :HEAD_WIDTH]
    value_piece = kv_all[..., HEAD_WIDTH:]
    scores = (
        jnp.einsum(
            "pshd,pnd->phsn", query_rows_normed, key_piece, preferred_element_type=jnp.float32
        )
        * score_scale
    )
    same_doc = segment_ids[:, :, None] == doc_all[:, None, :]
    probs = jnp.where(same_doc[:, None], jnp.exp(scores), jnp.float32(0.0))
    denom = jnp.sum(probs, axis=-1)
    probs_b = probs.astype(jnp.bfloat16)
    summed = jnp.einsum("phsn,pnd->pshd", probs_b, value_piece, preferred_element_type=jnp.float32)
    attn = (summed / jnp.transpose(denom, (0, 2, 1))[:, :, :, None]).astype(jnp.bfloat16)
    share = row_count // n_tp
    tp_index = lax.axis_index("tp")
    ep_index = lax.axis_index("ep")
    cp_index = lax.axis_index("cp")
    cap = capacity(share, top_count, experts)
    attn_pieces = cp_pieces(attn, n_cp)
    received_blocks = []
    for j, piece in enumerate(attn_pieces):
        if j > 0:
            piece, received_blocks[0] = lax.optimization_barrier((piece, received_blocks[0]))
        block = jnp.dot(
            piece.reshape(packs * row_count, head_count * HEAD_WIDTH),
            out_weight,
            preferred_element_type=jnp.float32,
        ).reshape(packs, row_count, out_weight.shape[1])
        summed = lax.psum_scatter(
            block.astype(jnp.bfloat16), "tp", scatter_dimension=1, tiled=True
        )
        if j > 0:
            summed = lax.ppermute(summed, "cp", [(i, (i - j) % n_cp) for i in range(n_cp)])
        received_blocks.append(summed)
    blocks = jnp.stack(received_blocks, axis=2).astype(jnp.float32)
    source_block = (jnp.arange(n_cp, dtype=jnp.int32) - cp_index) % n_cp
    picks_block = source_block[:, None] == jnp.arange(n_cp, dtype=jnp.int32)[None, :]
    projected = jnp.sum(
        jnp.where(picks_block[None, None, :, :, None], blocks[:, :, None, :, :], jnp.float32(0.0)),
        axis=3,
    ).reshape(packs, share, width)
    first_row = tp_index * share
    state = lax.dynamic_slice_in_dim(residual, first_row, share, 1).astype(jnp.float32) + projected
    local_ids = lax.dynamic_slice_in_dim(expert_ids, first_row, share, 1).reshape(
        packs * share, top_count
    )
    home_rows = packs * share
    normed = root_mean_scale(state.reshape(home_rows, width), norm_gain).astype(jnp.bfloat16)

    attn_pieces, expert_gate, expert_up, expert_down = lax.optimization_barrier(
        (attn_pieces, expert_gate, expert_up, expert_down)
    )
    gate_pieces = cp_pieces(expert_gate, n_cp)
    normed, gate_pieces = lax.optimization_barrier((normed, gate_pieces))
    up_down = jnp.concatenate([expert_up, expert_down], axis=2)
    gate_pieces, up_down = lax.optimization_barrier((gate_pieces, up_down))
    up_down_pieces = cp_pieces(up_down, n_cp)

    lanes = 128
    cap2 = n_ep * cap
    n_slots = n_tp * cap2
    gathered = n_ep * share
    row_iota = jnp.arange(gathered, dtype=jnp.int32)
    earlier = (row_iota[:, None] > row_iota[None, :]).astype(jnp.bfloat16)
    contract = (((0,), (0,)), ((), ()))
    id_lanes = jnp.pad(local_ids.astype(jnp.bfloat16), ((0, 0), (0, lanes - top_count)))
    rows_with_ids = jnp.concatenate([normed, id_lanes], axis=1)
    mixtures = []
    for chunk in range(packs):
        rows = rows_with_ids[chunk * share : (chunk + 1) * share]
        if chunk > 0:
            rows, _ = lax.optimization_barrier((rows, buffer))
        rows_all = lax.all_gather(rows, "ep", axis=0, tiled=True)
        normed_all = rows_all[:, :width]
        ids_all = rows_all[:, width : width + top_count].astype(jnp.int32)
        logits = jnp.dot(normed_all, router_weight, preferred_element_type=jnp.float32)
        picks = ids_all[:, :, None] == jnp.arange(experts, dtype=jnp.int32)[None, None, :]
        raised = jnp.exp(
            jnp.sum(jnp.where(picks, logits[:, None, :], jnp.float32(0.0)), axis=-1)
        )
        gates_all = raised / jnp.sum(raised, axis=-1, keepdims=True)
        mine = (ids_all % n_ep) == ep_index
        dest = ids_all // n_ep
        named = jnp.stack(
            [jnp.any(mine & (dest == j), axis=1) for j in range(n_tp)], axis=1
        ).astype(jnp.bfloat16)
        rank = jnp.dot(earlier, named, preferred_element_type=jnp.float32).astype(jnp.int32)
        rank_of = jnp.sum(
            jnp.where(dest[:, :, None] == jnp.arange(n_tp, dtype=jnp.int32)[None, None, :],
                      rank[:, None, :], 0),
            axis=-1,
        )
        target = jnp.where(mine, dest * cap2 + rank_of, jnp.int32(-1)).T
        if chunk == 0:
            full_gate = jnp.concatenate(gate_pieces, axis=2)
        hit = target[:, None, :] == jnp.arange(n_slots, dtype=jnp.int32)[None, :, None]
        select = jnp.any(hit, axis=0).astype(jnp.bfloat16)
        weight = jnp.sum(jnp.where(hit, gates_all.T[:, None, :], jnp.float32(0.0)), axis=0)

        buffer = jnp.dot(select, normed_all, preferred_element_type=jnp.float32).astype(
            jnp.bfloat16
        )
        received = lax.all_to_all(
            buffer.reshape(n_tp, cap2, width), "tp", split_axis=0, concat_axis=0, tiled=True
        )
        if chunk == 0:
            received, up_down_pieces = lax.optimization_barrier((received, up_down_pieces))
            units = expert_up.shape[2]
            full_up = jnp.concatenate([p[:, :, :units] for p in up_down_pieces], axis=2)
            full_down = jnp.concatenate([p[:, :, units:] for p in up_down_pieces], axis=2)
        served = expert_rows(received, full_gate, full_up, full_down)
        back = lax.all_to_all(served, "tp", split_axis=0, concat_axis=0, tiled=True).reshape(
            n_slots, width
        )

        weight_hi = weight.astype(jnp.bfloat16)
        weight_lo = (weight - weight_hi.astype(jnp.float32)).astype(jnp.bfloat16)
        partial = lax.dot_general(
            weight_hi, back, contract, preferred_element_type=jnp.float32
        ) + lax.dot_general(weight_lo, back, contract, preferred_element_type=jnp.float32)
        mixtures.append(
            lax.psum_scatter(
                partial.astype(jnp.bfloat16).reshape(n_ep, share, width),
                "ep",
                scatter_dimension=0,
                tiled=True,
            )
        )
    mixture = jnp.concatenate(mixtures, axis=0).astype(jnp.float32)
    layer_out = (state + mixture).astype(jnp.bfloat16)
    return layer_out


def solution(mesh):
    body = functools.partial(
        shards, n_cp=mesh.shape["cp"], n_tp=mesh.shape["tp"], n_ep=mesh.shape["ep"]
    )
    return jax.shard_map(
        body,
        mesh=mesh,
        in_specs=(
            P("ep", "cp", "tp"),
            P("ep", "cp", "tp"),
            P("ep", "cp", "tp"),
            P("ep", "cp"),
            P(),
            P(),
            P("tp", "cp"),
            P("ep", "cp", None),
            P(),
            P(),
            P("ep", "cp", None),
            P(("tp", "ep"), None, "cp"),
            P(("tp", "ep"), None, "cp"),
            P(("tp", "ep"), None, "cp"),
        ),
        out_specs=P("ep", ("cp", "tp"), None),
        check_vma=False,
    )
```
